256 devices in a mesh: dom: 64 (over z, x, core), sub: 4 (over y).
Axes of the slice: x: 4, y: 4, z: 8, core: 2. Of those that a mesh axis runs over, the one named last changes fastest.
Arguments:
- excitation: bfloat16 [64, 1536, 64], P('dom', 'sub'), may hold values from -6 to 6
- local_inverse: bfloat16 [64, 1536, 1536], P('dom', 'sub'), as said below
- aggregation: bfloat16 [64, 1024, 1536], P('dom', None, 'sub'), may hold values from -0.15625 to 0.15625
- disaggregation: bfloat16 [64, 1536, 1024], P('dom', 'sub'), may hold values from -0.1875 to 0.1875
- translation: float32 [64, 6, 2, 512], P('dom'), may hold values from -1.5 to 1.5
- partners: int32 [64, 6], P('dom'), may hold values from 0 to 63, as said below
- list_counts: int32 [64], P('dom'), may hold values from 2 to 6
- sweep_order: int32 [64], replicated, may hold values from 0 to 63, as said below
Outputs:
- currents: float32 [64, 1536, 64], P('dom', 'sub')
The draws below stay inside these ranges and needn't reach their ends.
Inputs may be any that keep to these rules, and one draw needn't show every extreme that they name: `partners`: row d names 6 different subdomains, none equal to d; only its first list_counts[d] slots are used. `local_inverse`: each subdomain's matrix is the identity plus independent entries of spread 0.6 / sqrt(1536). `sweep_order`: every subdomain has a position of its own.
All inputs are finite; a program needn't handle non-finite values.
Results may differ from the reference program's by a relative error of at most 0.03.
Values may be sent and summed in bfloat16 or wider, within the bound.
No kernel may reach another device: no remote copies, remote signals or barrier semaphores. Data moves between devices by JAX's collectives and lax.ppermute only.
A program may use at most 64 MiB of HBM per device.

```python
import jax
import jax.numpy as jnp
from jax import lax

U = 1536
R = 64
Q = 512
L = 6
SEGMENTS = 8
P2 = 1024
NDOM = 64


def draw_local_inverse(key, part):
    spread = 0.6 / U ** 0.5
    noise = jax.random.normal(key, (NDOM, U, U), jnp.float32)
    row_ids = jnp.arange(U, dtype=jnp.int32)
    identity = (row_ids[:, None] == row_ids[None, :]).astype(jnp.float32)
    return (identity[None, :, :] + spread * noise).astype(jnp.bfloat16)


def sweep_positions(key):
    return jax.random.permutation(jax.random.fold_in(key, 29), NDOM).astype(jnp.int32)


def draw_sweep_order(key, part):
    return sweep_positions(key)


def draw_partners(key, part):
    positions = sweep_positions(key)
    holders = jnp.argsort(positions).astype(jnp.int32)
    members = NDOM // SEGMENTS
    offsets = members + jnp.arange(L, dtype=jnp.int32)
    earlier = (positions[:, None] - offsets[None, :]) % NDOM
    return holders[earlier].astype(jnp.int32)


def plant(result, key, least, largest):
    shape = result.shape
    index_at = [jax.random.randint(jax.random.fold_in(key, axis), (), 0, shape[axis]) for axis in range(len(shape))]
    result = result.at[tuple(index_at)].set(least)
    longest = shape.index(max(shape))
    index_at[longest] = (index_at[longest] + 1) % shape[longest]
    return result.at[tuple(index_at)].set(largest)


def shard_levels(own_key, shape, shards, least, high):
    gain = 1.0
    for dim, shards_of in shards:
        heights = jax.random.uniform(jax.random.fold_in(jax.random.fold_in(own_key, 6), dim), (shards_of,), jnp.float32, least / len(shards), high / len(shards))
        gain = gain * jnp.repeat(jnp.exp(heights), shape[dim] // shards_of).reshape((-1,) + (1,) * (len(shape) - 1 - dim))
    return gain


def normal_values(own_key, shape, scale, bound, cuts=(), held_as=jnp.bfloat16):
    entries = jax.random.normal(own_key, shape, jnp.float32) * scale
    if len(cuts) > 0:
        entries = shard_levels(own_key, shape, cuts, -0.22, 0.18) * entries
    return jnp.clip(entries, min=-bound, max=bound).astype(held_as)


def setup_inputs(seed: int = 0) -> dict:
    key_list = jax.random.split(jax.random.key(seed), 9)
    return {
        "excitation": normal_values(key_list[0], (NDOM, U, R), 1.0, 6.0, ((0, 64), (1, 4))),
        "local_inverse": draw_local_inverse(jax.random.fold_in(key_list[8], 71), 0),
        "aggregation": normal_values(key_list[2], (NDOM, P2, U), U ** -0.5, 0.15625, ((0, 64), (2, 4))),
        "disaggregation": normal_values(key_list[3], (NDOM, U, P2), P2 ** -0.5, 0.1875, ((0, 64), (1, 4))),
        "translation": normal_values(key_list[4], (NDOM, L, 2, Q), 0.3, 1.5, ((0, 64),), jnp.float32),
        "partners": draw_partners(jax.random.fold_in(key_list[8], 71), 0),
        "list_counts": plant(jax.random.randint(key_list[6], (NDOM,), 2, L + 1), jax.random.fold_in(key_list[6], 1), 2, L).astype(jnp.int32),
        "sweep_order": draw_sweep_order(jax.random.fold_in(key_list[8], 71), 0),
    }


CONTRACT_FIRST = (((0,), (1,)), ((), ()))
CONTRACT_LAST = (((1,), (1,)), ((), ()))


def rotate(real_weight, imag_weight, pattern):
    samples = real_weight.shape[-1]
    values = pattern.astype(jnp.float32)
    real_part = values[..., :samples]
    imag_part = values[..., samples:]
    return jnp.concatenate([real_weight * real_part - imag_weight * imag_part, real_weight * imag_part + imag_weight * real_part], axis=-1)


def prepare(blocks):
    inverse_block, disagg_block, agg_block, excite_block = blocks
    solved = jnp.dot(inverse_block, excite_block, preferred_element_type=jnp.float32)
    solved_half = solved.astype(jnp.bfloat16)
    incident = lax.dot_general(solved_half, agg_block, CONTRACT_FIRST, preferred_element_type=jnp.float32)
    spread_half = jnp.dot(inverse_block, disagg_block, preferred_element_type=jnp.float32).astype(jnp.bfloat16)
    coupling = lax.dot_general(spread_half, agg_block, CONTRACT_FIRST, preferred_element_type=jnp.float32).astype(jnp.bfloat16)
    return solved, incident, spread_half, coupling


def finish(blocks):
    solved_block, spread_block, field_block = blocks
    return solved_block - lax.dot_general(spread_block, field_block, CONTRACT_LAST, preferred_element_type=jnp.float32)


def reference(excitation, local_inverse, aggregation, disaggregation, translation, partners, list_counts, sweep_order):
    solved, incident, spread_half, coupling = lax.map(prepare, (local_inverse, disaggregation, aggregation, excitation))
    domains = sweep_order.shape[0]
    segment_of = (sweep_order * SEGMENTS) // domains
    slot_ids = jnp.arange(partners.shape[1], dtype=jnp.int32)
    patterns = jnp.zeros(incident.shape, jnp.bfloat16)
    fields = jnp.zeros(incident.shape, jnp.bfloat16)
    for segment_k in range(SEGMENTS):
        live = (slot_ids[None, :] < list_counts[:, None]) & (segment_of[partners] < segment_k)
        weights = jnp.where(live[:, :, None, None], translation, jnp.zeros_like(translation))

        def gather_field(blocks):
            weight_block, linked = blocks
            terms = rotate(weight_block[:, 0][:, None, :], weight_block[:, 1][:, None, :], patterns[linked])
            return jnp.sum(terms, axis=0).astype(jnp.bfloat16)

        now_fields = lax.map(gather_field, (weights, partners))

        def radiate(blocks):
            field_block, incident_block, coupling_block = blocks
            return (incident_block - jnp.dot(field_block, coupling_block, preferred_element_type=jnp.float32)).astype(jnp.bfloat16)

        now_patterns = lax.map(radiate, (now_fields, incident, coupling))
        in_segment = (segment_of == segment_k)[:, None, None]
        fields = jnp.where(in_segment, now_fields, fields)
        patterns = jnp.where(in_segment, now_patterns, patterns)
    return lax.map(finish, (solved, spread_half, fields))
```

```python
import jax
import jax.numpy as jnp
from jax import lax
from jax.sharding import Mesh
from jax.sharding import PartitionSpec as P

SEGMENTS = 8
CORES = 2


CONTRACT_FIRST = (((0,), (1,)), ((), ()))
CONTRACT_LAST = (((1,), (1,)), ((), ()))
DOM = ("zx", "core")


def rotate(real_weight, imag_weight, pattern):
    samples = real_weight.shape[-1]
    values = pattern.astype(jnp.float32)
    real_part = values[..., :samples]
    imag_part = values[..., samples:]
    return jnp.concatenate(
        [
            real_weight * real_part - imag_weight * imag_part,
            real_weight * imag_part + imag_weight * real_part,
        ],
        axis=-1,
    )


def share_slots(slots, chips):
    shape = slots.shape
    swap = [(0, 1), (1, 0)]
    slots = slots + lax.ppermute(slots, "core", swap)
    core = lax.axis_index("core")
    halves = slots.reshape(CORES, -1)
    mine = lax.dynamic_index_in_dim(halves, core, 0, keepdims=False).reshape(chips, -1)
    pieces = lax.all_to_all(mine, "zx", 0, 0, tiled=True)
    total = jnp.sum(pieces, axis=0, keepdims=True)
    spread = jnp.broadcast_to(total, (chips, total.shape[1]))
    gathered = lax.all_to_all(spread, "zx", 0, 0, tiled=True).reshape(-1)
    other = lax.ppermute(gathered, "core", swap)
    whole = jnp.where(
        core == 0,
        jnp.concatenate([gathered, other]),
        jnp.concatenate([other, gathered]),
    )
    return whole.reshape(shape)


def local(
    excitation,
    local_inverse,
    aggregation,
    disaggregation,
    translation,
    partners,
    list_counts,
    sweep_order,
):
    chips = lax.axis_size("zx")
    excite_rows = excitation[0]
    inverse_rows = local_inverse[0]
    agg_columns = aggregation[0]
    disagg_rows = disaggregation[0]
    trans_rows = translation[0]
    partner_row = partners[0]

    def apply_inverse(shard_rows):
        return jnp.dot(inverse_rows, shard_rows, preferred_element_type=jnp.float32)

    solved = apply_inverse(lax.all_gather(excite_rows, "sub", axis=0, tiled=True))
    solved_half = solved.astype(jnp.bfloat16)
    incident = lax.psum_scatter(
        lax.dot_general(
            solved_half, agg_columns, CONTRACT_FIRST, preferred_element_type=jnp.float32
        ).astype(jnp.bfloat16),
        "sub",
        scatter_dimension=0,
        tiled=True,
    ).astype(jnp.float32)
    spread = apply_inverse(lax.all_gather(disagg_rows, "sub", axis=0, tiled=True))
    spread_half = spread.astype(jnp.bfloat16)
    partial_map = lax.dot_general(
        spread_half, agg_columns, CONTRACT_FIRST, preferred_element_type=jnp.float32
    )
    coupling = lax.psum(partial_map.astype(jnp.bfloat16), "sub")

    domains = sweep_order.shape[0]
    members = domains // SEGMENTS
    segment_of = sweep_order * SEGMENTS // domains
    own_index = lax.axis_index("zx") * CORES + lax.axis_index("core")
    my_segment = segment_of[own_index]
    my_slot = sweep_order[own_index] - my_segment * members
    slot_ids = jnp.arange(members, dtype=jnp.int32)
    slot_live = jnp.arange(partner_row.shape[0], dtype=jnp.int32) < list_counts[0]
    partner_pos = sweep_order[partner_row]
    partner_segment = partner_pos * SEGMENTS // domains
    partner_slot = partner_pos - partner_segment * members

    incoming = jnp.zeros(incident.shape, jnp.float32)
    for segment_k in range(SEGMENTS - 1):
        pattern = (
            incident
            - jnp.dot(incoming.astype(jnp.bfloat16), coupling, preferred_element_type=jnp.float32)
        ).astype(jnp.bfloat16)
        mine = (slot_ids == my_slot) & (my_segment == segment_k)
        slots = jnp.where(mine[:, None, None], pattern[None], jnp.zeros_like(pattern)[None])
        slots = share_slots(slots, chips)
        match = (
            (partner_slot[:, None] == slot_ids[None, :])
            & (partner_segment[:, None] == segment_k)
            & slot_live[:, None]
            & (segment_k < my_segment)
        )
        weights = jnp.sum(
            jnp.where(match[:, :, None, None], trans_rows[:, None, :, :], 0.0), axis=0
        )
        terms = rotate(weights[:, 0][:, None, :], weights[:, 1][:, None, :], slots)
        incoming = incoming + jnp.sum(terms, axis=0)
    fields = lax.all_gather(incoming.astype(jnp.bfloat16), "sub", axis=0, tiled=True)
    currents = solved - lax.dot_general(
        spread_half, fields, CONTRACT_LAST, preferred_element_type=jnp.float32
    )
    return currents[None]


def solution(mesh):
    dom_size, sub_size = mesh.devices.shape
    fine = Mesh(mesh.devices.reshape(dom_size // CORES, CORES, sub_size), ("zx", "core", "sub"))
    in_specs = (
        P(DOM, "sub", None),
        P(DOM, "sub", None),
        P(DOM, None, "sub"),
        P(DOM, "sub", None),
        P(DOM, None, None, None),
        P(DOM, None),
        P(DOM),
        P(),
    )
    out_specs = P(DOM, "sub", None)
    return jax.shard_map(local, mesh=fine, in_specs=in_specs, out_specs=out_specs, check_vma=False)
```

```python
import jax
import jax.numpy as jnp
from jax import lax
from jax.sharding import Mesh
from jax.sharding import PartitionSpec as P

SEGMENTS = 8
CORES = 2


CONTRACT_FIRST = (((0,), (1,)), ((), ()))
CONTRACT_LAST = (((1,), (1,)), ((), ()))
DOM = ("zx", "core")
LANES = 128


def to_tiles(rows):
    lead = rows.shape[:-2]
    count, width = rows.shape[-2:]
    tiled = rows.reshape(lead + (count, width // LANES, LANES))
    return jnp.moveaxis(tiled, -2, -3)


def from_tiles(tiles):
    lead = tiles.shape[:-3]
    groups, count, lanes = tiles.shape[-3:]
    return jnp.moveaxis(tiles, -3, -2).reshape(lead + (count, groups * lanes))


def share_slots(slots, chips):
    swap = [(0, 1), (1, 0)]
    slots = slots + lax.ppermute(slots, "core", swap)
    core = lax.axis_index("core")
    count = slots.shape[0]
    halves = slots.reshape((CORES, count // CORES) + slots.shape[1:])
    mine = lax.dynamic_index_in_dim(halves, core, 0, keepdims=False)
    tile_shape = mine.shape[2:]
    pieces = lax.all_to_all(mine.reshape((chips,) + tile_shape), "zx", 0, 0, tiled=True)
    total = jnp.sum(pieces, axis=0, keepdims=True)
    spread = jnp.broadcast_to(total, (chips,) + tile_shape)
    gathered = lax.all_to_all(spread, "zx", 0, 0, tiled=True).reshape(mine.shape)
    other = lax.ppermute(gathered, "core", swap)
    return jnp.where(
        core == 0,
        jnp.concatenate([gathered, other]),
        jnp.concatenate([other, gathered]),
    )


def local(
    excitation,
    local_inverse,
    aggregation,
    disaggregation,
    translation,
    partners,
    list_counts,
    sweep_order,
):
    chips = lax.axis_size("zx")
    excite_rows = excitation[0]
    inverse_rows = local_inverse[0]
    agg_columns = aggregation[0]
    disagg_rows = disaggregation[0]
    trans_rows = translation[0]
    partner_row = partners[0]

    def apply_inverse(shard_rows):
        return jnp.dot(inverse_rows, shard_rows, preferred_element_type=jnp.float32)

    solved = apply_inverse(lax.all_gather(excite_rows, "sub", axis=0, tiled=True))
    solved_half = solved.astype(jnp.bfloat16)
    incident = lax.psum_scatter(
        lax.dot_general(
            solved_half, agg_columns, CONTRACT_FIRST, preferred_element_type=jnp.float32
        ).astype(jnp.bfloat16),
        "sub",
        scatter_dimension=0,
        tiled=True,
    ).astype(jnp.float32)
    spread = apply_inverse(lax.all_gather(disagg_rows, "sub", axis=0, tiled=True))
    spread_half = spread.astype(jnp.bfloat16)
    partial_map = lax.dot_general(
        spread_half, agg_columns, CONTRACT_FIRST, preferred_element_type=jnp.float32
    )
    coupling = lax.psum(partial_map.astype(jnp.bfloat16), "sub")

    domains = sweep_order.shape[0]
    members = domains // SEGMENTS
    segment_of = sweep_order * SEGMENTS // domains
    own_index = lax.axis_index("zx") * CORES + lax.axis_index("core")
    my_segment = segment_of[own_index]
    my_slot = sweep_order[own_index] - my_segment * members
    slot_ids = jnp.arange(members, dtype=jnp.int32)
    slot_live = jnp.arange(partner_row.shape[0], dtype=jnp.int32) < list_counts[0]
    partner_pos = sweep_order[partner_row]
    partner_segment = partner_pos * SEGMENTS // domains
    partner_slot = partner_pos - partner_segment * members

    half_samples = trans_rows.shape[-1] // LANES
    trans_tiles = trans_rows.reshape(trans_rows.shape[:2] + (half_samples, 1, LANES))
    incoming = jnp.zeros(to_tiles(incident).shape, jnp.float32)
    for segment_k in range(SEGMENTS - 1):
        if segment_k == 0:
            pattern = incident.astype(jnp.bfloat16)
        else:
            pattern = (
                incident
                - jnp.dot(
                    from_tiles(incoming).astype(jnp.bfloat16),
                    coupling,
                    preferred_element_type=jnp.float32,
                )
            ).astype(jnp.bfloat16)
        mine = (slot_ids == my_slot) & (my_segment == segment_k)
        pattern_tiles = to_tiles(pattern)
        slots = jnp.where(
            mine[:, None, None, None], pattern_tiles[None], jnp.zeros_like(pattern_tiles)[None]
        )
        slots = share_slots(slots, chips).astype(jnp.float32)
        match = (
            (partner_slot[:, None] == slot_ids[None, :])
            & (partner_segment[:, None] == segment_k)
            & slot_live[:, None]
            & (segment_k < my_segment)
        )
        weights = jnp.sum(
            jnp.where(match[:, :, None, None, None, None], trans_tiles[:, None], 0.0), axis=0
        )
        real_weight = weights[:, 0]
        imag_weight = weights[:, 1]
        real_part = slots[:, :half_samples]
        imag_part = slots[:, half_samples:]
        incoming = incoming + jnp.concatenate(
            [
                jnp.sum(real_weight * real_part - imag_weight * imag_part, axis=0),
                jnp.sum(real_weight * imag_part + imag_weight * real_part, axis=0),
            ],
            axis=0,
        )
    incoming = from_tiles(incoming)
    fields = lax.all_gather(incoming.astype(jnp.bfloat16), "sub", axis=0, tiled=True)
    currents = solved - lax.dot_general(
        spread_half, fields, CONTRACT_LAST, preferred_element_type=jnp.float32
    )
    return currents[None]


def solution(mesh):
    dom_size, sub_size = mesh.devices.shape
    fine = Mesh(mesh.devices.reshape(dom_size // CORES, CORES, sub_size), ("zx", "core", "sub"))
    in_specs = (
        P(DOM, "sub", None),
        P(DOM, "sub", None),
        P(DOM, None, "sub"),
        P(DOM, "sub", None),
        P(DOM, None, None, None),
        P(DOM, None),
        P(DOM),
        P(),
    )
    out_specs = P(DOM, "sub", None)
    return jax.shard_map(local, mesh=fine, in_specs=in_specs, out_specs=out_specs, check_vma=False)
```

```python
import jax
import jax.numpy as jnp
from jax import lax
from jax.sharding import Mesh
from jax.sharding import PartitionSpec as P

SEGMENTS = 8
CORES = 2


CONTRACT_FIRST = (((0,), (1,)), ((), ()))
CONTRACT_LAST = (((1,), (1,)), ((), ()))
DOM = ("zx", "core")
LANES = 128


def to_tiles(rows):
    lead = rows.shape[:-2]
    count, width = rows.shape[-2:]
    tiled = rows.reshape(lead + (count, width // LANES, LANES))
    return jnp.moveaxis(tiled, -2, -3)


def from_tiles(tiles):
    lead = tiles.shape[:-3]
    groups, count, lanes = tiles.shape[-3:]
    return jnp.moveaxis(tiles, -3, -2).reshape(lead + (count, groups * lanes))


def share_slots(slots, chips):
    swap = [(0, 1), (1, 0)]
    slots = slots + lax.ppermute(slots, "core", swap)
    core = lax.axis_index("core")
    count = slots.shape[0]
    halves = slots.reshape((CORES, count // CORES) + slots.shape[1:])
    mine = lax.dynamic_index_in_dim(halves, core, 0, keepdims=False)
    tile_shape = mine.shape[2:]
    pieces = lax.all_to_all(mine.reshape((chips,) + tile_shape), "zx", 0, 0, tiled=True)
    total = jnp.sum(pieces, axis=0, keepdims=True)
    spread = jnp.broadcast_to(total, (chips,) + tile_shape)
    gathered = lax.all_to_all(spread, "zx", 0, 0, tiled=True).reshape(mine.shape)
    other = lax.ppermute(gathered, "core", swap)
    return jnp.where(
        core == 0,
        jnp.concatenate([gathered, other]),
        jnp.concatenate([other, gathered]),
    )


def gather_rows(rows, subs):
    copies = jnp.broadcast_to(rows[None], (subs,) + rows.shape)
    pieces = lax.all_to_all(copies, "sub", 0, 0, tiled=True)
    return pieces.reshape((subs * rows.shape[0],) + rows.shape[1:])


def local(
    excitation,
    local_inverse,
    aggregation,
    disaggregation,
    translation,
    partners,
    list_counts,
    sweep_order,
):
    chips = lax.axis_size("zx")
    excite_rows = excitation[0]
    inverse_rows = local_inverse[0]
    agg_columns = aggregation[0]
    disagg_rows = disaggregation[0]
    trans_rows = translation[0]
    partner_row = partners[0]

    def apply_inverse(shard_rows):
        return jnp.dot(inverse_rows, shard_rows, preferred_element_type=jnp.float32)

    subs = lax.axis_size("sub")
    solved = apply_inverse(gather_rows(excite_rows, subs))
    solved_half = solved.astype(jnp.bfloat16)
    partial_incident = lax.dot_general(
        solved_half, agg_columns, CONTRACT_FIRST, preferred_element_type=jnp.float32
    ).astype(jnp.bfloat16)
    incident_pieces = lax.all_to_all(
        partial_incident.reshape((subs, -1) + partial_incident.shape[1:]), "sub", 0, 0, tiled=True
    )
    incident = jnp.sum(incident_pieces.astype(jnp.float32), axis=0)
    spread = apply_inverse(lax.all_gather(disagg_rows, "sub", axis=0, tiled=True))
    spread_half = spread.astype(jnp.bfloat16)
    partial_map = lax.dot_general(
        spread_half, agg_columns, CONTRACT_FIRST, preferred_element_type=jnp.float32
    )
    coupling = lax.psum(partial_map.astype(jnp.bfloat16), "sub")

    domains = sweep_order.shape[0]
    members = domains // SEGMENTS
    segment_of = sweep_order * SEGMENTS // domains
    own_index = lax.axis_index("zx") * CORES + lax.axis_index("core")
    my_segment = segment_of[own_index]
    my_slot = sweep_order[own_index] - my_segment * members
    slot_ids = jnp.arange(members, dtype=jnp.int32)
    slot_live = jnp.arange(partner_row.shape[0], dtype=jnp.int32) < list_counts[0]
    partner_pos = sweep_order[partner_row]
    partner_segment = partner_pos * SEGMENTS // domains
    partner_slot = partner_pos - partner_segment * members

    half_samples = trans_rows.shape[-1] // LANES
    trans_tiles = trans_rows.reshape(trans_rows.shape[:2] + (half_samples, 1, LANES))
    incoming = jnp.zeros(to_tiles(incident).shape, jnp.float32)
    for segment_k in range(SEGMENTS - 1):
        if segment_k == 0:
            pattern = incident.astype(jnp.bfloat16)
        else:
            pattern = (
                incident
                - jnp.dot(
                    from_tiles(incoming).astype(jnp.bfloat16),
                    coupling,
                    preferred_element_type=jnp.float32,
                )
            ).astype(jnp.bfloat16)
        mine = (slot_ids == my_slot) & (my_segment == segment_k)
        pattern_tiles = to_tiles(pattern)
        slots = jnp.where(
            mine[:, None, None, None], pattern_tiles[None], jnp.zeros_like(pattern_tiles)[None]
        )
        slots = share_slots(slots, chips).astype(jnp.float32)
        match = (
            (partner_slot[:, None] == slot_ids[None, :])
            & (partner_segment[:, None] == segment_k)
            & slot_live[:, None]
            & (segment_k < my_segment)
        )
        weights = jnp.sum(
            jnp.where(match[:, :, None, None, None, None], trans_tiles[:, None], 0.0), axis=0
        )
        real_weight = weights[:, 0]
        imag_weight = weights[:, 1]
        real_part = slots[:, :half_samples]
        imag_part = slots[:, half_samples:]
        incoming = incoming + jnp.concatenate(
            [
                jnp.sum(real_weight * real_part - imag_weight * imag_part, axis=0),
                jnp.sum(real_weight * imag_part + imag_weight * real_part, axis=0),
            ],
            axis=0,
        )
    incoming = from_tiles(incoming)
    fields = gather_rows(incoming.astype(jnp.bfloat16), subs)
    currents = solved - lax.dot_general(
        spread_half, fields, CONTRACT_LAST, preferred_element_type=jnp.float32
    )
    return currents[None]


def solution(mesh):
    dom_size, sub_size = mesh.devices.shape
    fine = Mesh(mesh.devices.reshape(dom_size // CORES, CORES, sub_size), ("zx", "core", "sub"))
    in_specs = (
        P(DOM, "sub", None),
        P(DOM, "sub", None),
        P(DOM, None, "sub"),
        P(DOM, "sub", None),
        P(DOM, None, None, None),
        P(DOM, None),
        P(DOM),
        P(),
    )
    out_specs = P(DOM, "sub", None)
    return jax.shard_map(local, mesh=fine, in_specs=in_specs, out_specs=out_specs, check_vma=False)
```

```python
import jax
import jax.numpy as jnp
from jax import lax
from jax.sharding import Mesh
from jax.sharding import PartitionSpec as P

SEGMENTS = 8
CORES = 2


CONTRACT_FIRST = (((0,), (1,)), ((), ()))
CONTRACT_LAST = (((1,), (1,)), ((), ()))
DOM = ("zx", "core")
LANES = 128


def to_tiles(rows):
    lead = rows.shape[:-2]
    count, width = rows.shape[-2:]
    tiled = rows.reshape(lead + (count, width // LANES, LANES))
    return jnp.moveaxis(tiled, -2, -3)


def from_tiles(tiles):
    lead = tiles.shape[:-3]
    groups, count, lanes = tiles.shape[-3:]
    return jnp.moveaxis(tiles, -3, -2).reshape(lead + (count, groups * lanes))


def share_slots(slots, chips):
    swap = [(0, 1), (1, 0)]
    slots = slots + lax.ppermute(slots, "core", swap)
    core = lax.axis_index("core")
    count = slots.shape[0]
    halves = slots.reshape((CORES, count // CORES) + slots.shape[1:])
    mine = lax.dynamic_index_in_dim(halves, core, 0, keepdims=False)
    tile_shape = mine.shape[2:]
    pieces = lax.all_to_all(mine.reshape((chips,) + tile_shape), "zx", 0, 0, tiled=True)
    total = jnp.sum(pieces, axis=0, keepdims=True)
    spread = jnp.broadcast_to(total, (chips,) + tile_shape)
    gathered = lax.all_to_all(spread, "zx", 0, 0, tiled=True).reshape(mine.shape)
    other = lax.ppermute(gathered, "core", swap)
    return jnp.where(
        core == 0,
        jnp.concatenate([gathered, other]),
        jnp.concatenate([other, gathered]),
    )


def gather_rows(rows, subs):
    copies = jnp.broadcast_to(rows[None], (subs,) + rows.shape)
    pieces = lax.all_to_all(copies, "sub", 0, 0, tiled=True)
    return pieces.reshape((subs * rows.shape[0],) + rows.shape[1:])


def local(
    excitation,
    local_inverse,
    aggregation,
    disaggregation,
    translation,
    partners,
    list_counts,
    sweep_order,
):
    chips = lax.axis_size("zx")
    excite_rows = excitation[0]
    inverse_rows = local_inverse[0]
    agg_columns = aggregation[0]
    disagg_rows = disaggregation[0]
    trans_rows = translation[0]
    partner_row = partners[0]

    def apply_inverse(shard_rows):
        return jnp.dot(inverse_rows, shard_rows, preferred_element_type=jnp.float32)

    subs = lax.axis_size("sub")
    solved = apply_inverse(gather_rows(excite_rows, subs))
    solved_half = solved.astype(jnp.bfloat16)
    partial_incident = lax.dot_general(
        solved_half, agg_columns, CONTRACT_FIRST, preferred_element_type=jnp.float32
    ).astype(jnp.bfloat16)
    incident_pieces = lax.all_to_all(
        partial_incident.reshape((subs, -1) + partial_incident.shape[1:]), "sub", 0, 0, tiled=True
    )
    incident = jnp.sum(incident_pieces.astype(jnp.float32), axis=0)
    sub_index = lax.axis_index("sub")
    block = disagg_rows.shape[0]
    spread = jnp.zeros((inverse_rows.shape[0], disagg_rows.shape[1]), jnp.float32)
    for hop in range(subs):
        if hop == 0:
            rows = disagg_rows
        else:
            rows = lax.ppermute(disagg_rows, "sub", [(i, i ^ hop) for i in range(subs)])
        columns = lax.dynamic_slice_in_dim(inverse_rows, (sub_index ^ hop) * block, block, axis=1)
        spread = spread + jnp.dot(columns, rows, preferred_element_type=jnp.float32)
    spread_half = spread.astype(jnp.bfloat16)
    partial_map = lax.dot_general(
        spread_half, agg_columns, CONTRACT_FIRST, preferred_element_type=jnp.float32
    ).astype(jnp.bfloat16)
    map_pieces = lax.all_to_all(
        partial_map.reshape((subs, -1) + partial_map.shape[1:]), "sub", 0, 0, tiled=True
    )
    map_share = jnp.sum(map_pieces.astype(jnp.float32), axis=0).astype(jnp.bfloat16)
    coupling = gather_rows(map_share, subs)

    domains = sweep_order.shape[0]
    members = domains // SEGMENTS
    segment_of = sweep_order * SEGMENTS // domains
    own_index = lax.axis_index("zx") * CORES + lax.axis_index("core")
    my_segment = segment_of[own_index]
    my_slot = sweep_order[own_index] - my_segment * members
    slot_ids = jnp.arange(members, dtype=jnp.int32)
    slot_live = jnp.arange(partner_row.shape[0], dtype=jnp.int32) < list_counts[0]
    partner_pos = sweep_order[partner_row]
    partner_segment = partner_pos * SEGMENTS // domains
    partner_slot = partner_pos - partner_segment * members

    half_samples = trans_rows.shape[-1] // LANES
    trans_tiles = trans_rows.reshape(trans_rows.shape[:2] + (half_samples, 1, LANES))
    incoming = jnp.zeros(to_tiles(incident).shape, jnp.float32)
    for segment_k in range(SEGMENTS - 1):
        if segment_k == 0:
            pattern = incident.astype(jnp.bfloat16)
        else:
            pattern = (
                incident
                - jnp.dot(
                    from_tiles(incoming).astype(jnp.bfloat16),
                    coupling,
                    preferred_element_type=jnp.float32,
                )
            ).astype(jnp.bfloat16)
        mine = (slot_ids == my_slot) & (my_segment == segment_k)
        pattern_tiles = to_tiles(pattern)
        slots = jnp.where(
            mine[:, None, None, None], pattern_tiles[None], jnp.zeros_like(pattern_tiles)[None]
        )
        slots = share_slots(slots, chips).astype(jnp.float32)
        match = (
            (partner_slot[:, None] == slot_ids[None, :])
            & (partner_segment[:, None] == segment_k)
            & slot_live[:, None]
            & (segment_k < my_segment)
        )
        weights = jnp.sum(
            jnp.where(match[:, :, None, None, None, None], trans_tiles[:, None], 0.0), axis=0
        )
        real_weight = weights[:, 0]
        imag_weight = weights[:, 1]
        real_part = slots[:, :half_samples]
        imag_part = slots[:, half_samples:]
        incoming = incoming + jnp.concatenate(
            [
                jnp.sum(real_weight * real_part - imag_weight * imag_part, axis=0),
                jnp.sum(real_weight * imag_part + imag_weight * real_part, axis=0),
            ],
            axis=0,
        )
    incoming = from_tiles(incoming)
    fields = gather_rows(incoming.astype(jnp.bfloat16), subs)
    currents = solved - lax.dot_general(
        spread_half, fields, CONTRACT_LAST, preferred_element_type=jnp.float32
    )
    return currents[None]


def solution(mesh):
    dom_size, sub_size = mesh.devices.shape
    fine = Mesh(mesh.devices.reshape(dom_size // CORES, CORES, sub_size), ("zx", "core", "sub"))
    in_specs = (
        P(DOM, "sub", None),
        P(DOM, "sub", None),
        P(DOM, None, "sub"),
        P(DOM, "sub", None),
        P(DOM, None, None, None),
        P(DOM, None),
        P(DOM),
        P(),
    )
    out_specs = P(DOM, "sub", None)
    return jax.shard_map(local, mesh=fine, in_specs=in_specs, out_specs=out_specs, check_vma=False)
```

```python
import jax
import jax.numpy as jnp
from jax import lax
from jax.sharding import Mesh
from jax.sharding import PartitionSpec as P

SEGMENTS = 8
CORES = 2


CONTRACT_FIRST = (((0,), (1,)), ((), ()))
CONTRACT_LAST = (((1,), (1,)), ((), ()))
DOM = ("zx", "core")
LANES = 128


def to_tiles(rows):
    lead = rows.shape[:-2]
    count, width = rows.shape[-2:]
    tiled = rows.reshape(lead + (count, width // LANES, LANES))
    return jnp.moveaxis(tiled, -2, -3)


def from_tiles(tiles):
    lead = tiles.shape[:-3]
    groups, count, lanes = tiles.shape[-3:]
    return jnp.moveaxis(tiles, -3, -2).reshape(lead + (count, groups * lanes))


def share_slots(slots, chips):
    shape = slots.shape
    tile_shape = shape[-2:]
    per_chip = slots.reshape((chips, -1) + tile_shape)
    pieces = lax.all_to_all(per_chip, "zx", 0, 0, tiled=True)
    total = jnp.sum(pieces, axis=0)
    total = total + lax.ppermute(total, "core", [(0, 1), (1, 0)])
    spread = jnp.broadcast_to(total[None], per_chip.shape)
    gathered = lax.all_to_all(spread, "zx", 0, 0, tiled=True)
    return gathered.reshape(shape)


def gather_rows(rows, subs):
    copies = jnp.broadcast_to(rows[None], (subs,) + rows.shape)
    pieces = lax.all_to_all(copies, "sub", 0, 0, tiled=True)
    return pieces.reshape((subs * rows.shape[0],) + rows.shape[1:])


def local(
    excitation,
    local_inverse,
    aggregation,
    disaggregation,
    translation,
    partners,
    list_counts,
    sweep_order,
):
    chips = lax.axis_size("zx")
    excite_rows = excitation[0]
    inverse_rows = local_inverse[0]
    agg_columns = aggregation[0]
    disagg_rows = disaggregation[0]
    trans_rows = translation[0]
    partner_row = partners[0]

    def apply_inverse(shard_rows):
        return jnp.dot(inverse_rows, shard_rows, preferred_element_type=jnp.float32)

    subs = lax.axis_size("sub")
    solved = apply_inverse(gather_rows(excite_rows, subs))
    solved_half = solved.astype(jnp.bfloat16)
    partial_incident = lax.dot_general(
        solved_half, agg_columns, CONTRACT_FIRST, preferred_element_type=jnp.float32
    ).astype(jnp.bfloat16)
    incident_pieces = lax.all_to_all(
        partial_incident.reshape((subs, -1) + partial_incident.shape[1:]), "sub", 0, 0, tiled=True
    )
    incident = jnp.sum(incident_pieces.astype(jnp.float32), axis=0)
    spread = apply_inverse(lax.all_gather(disagg_rows, "sub", axis=0, tiled=True))
    spread_half = spread.astype(jnp.bfloat16)
    partial_map = lax.dot_general(
        spread_half, agg_columns, CONTRACT_FIRST, preferred_element_type=jnp.float32
    )
    coupling = lax.psum(partial_map.astype(jnp.bfloat16), "sub")

    domains = sweep_order.shape[0]
    members = domains // SEGMENTS
    segment_of = sweep_order * SEGMENTS // domains
    own_index = lax.axis_index("zx") * CORES + lax.axis_index("core")
    my_segment = segment_of[own_index]
    my_slot = sweep_order[own_index] - my_segment * members
    slot_ids = jnp.arange(members, dtype=jnp.int32)
    slot_live = jnp.arange(partner_row.shape[0], dtype=jnp.int32) < list_counts[0]
    partner_pos = sweep_order[partner_row]
    partner_segment = partner_pos * SEGMENTS // domains
    partner_slot = partner_pos - partner_segment * members

    half_samples = trans_rows.shape[-1] // LANES
    trans_tiles = trans_rows.reshape(trans_rows.shape[:2] + (half_samples, 1, LANES))
    incoming = jnp.zeros(to_tiles(incident).shape, jnp.float32)
    for segment_k in range(SEGMENTS - 1):
        if segment_k == 0:
            pattern = incident.astype(jnp.bfloat16)
        else:
            pattern = (
                incident
                - jnp.dot(
                    from_tiles(incoming).astype(jnp.bfloat16),
                    coupling,
                    preferred_element_type=jnp.float32,
                )
            ).astype(jnp.bfloat16)
        mine = (slot_ids == my_slot) & (my_segment == segment_k)
        pattern_tiles = to_tiles(pattern)
        slots = jnp.where(
            mine[:, None, None, None], pattern_tiles[None], jnp.zeros_like(pattern_tiles)[None]
        )
        slots = share_slots(slots, chips).astype(jnp.float32)
        match = (
            (partner_slot[:, None] == slot_ids[None, :])
            & (partner_segment[:, None] == segment_k)
            & slot_live[:, None]
            & (segment_k < my_segment)
        )
        weights = jnp.sum(
            jnp.where(match[:, :, None, None, None, None], trans_tiles[:, None], 0.0), axis=0
        )
        real_weight = weights[:, 0]
        imag_weight = weights[:, 1]
        real_part = slots[:, :half_samples]
        imag_part = slots[:, half_samples:]
        incoming = incoming + jnp.concatenate(
            [
                jnp.sum(real_weight * real_part - imag_weight * imag_part, axis=0),
                jnp.sum(real_weight * imag_part + imag_weight * real_part, axis=0),
            ],
            axis=0,
        )
    incoming = from_tiles(incoming)
    fields = gather_rows(incoming.astype(jnp.bfloat16), subs)
    currents = solved - lax.dot_general(
        spread_half, fields, CONTRACT_LAST, preferred_element_type=jnp.float32
    )
    return currents[None]


def solution(mesh):
    dom_size, sub_size = mesh.devices.shape
    fine = Mesh(mesh.devices.reshape(dom_size // CORES, CORES, sub_size), ("zx", "core", "sub"))
    in_specs = (
        P(DOM, "sub", None),
        P(DOM, "sub", None),
        P(DOM, None, "sub"),
        P(DOM, "sub", None),
        P(DOM, None, None, None),
        P(DOM, None),
        P(DOM),
        P(),
    )
    out_specs = P(DOM, "sub", None)
    return jax.shard_map(local, mesh=fine, in_specs=in_specs, out_specs=out_specs, check_vma=False)
```

```python
import jax
import jax.numpy as jnp
from jax import lax
from jax.sharding import Mesh
from jax.sharding import PartitionSpec as P

SEGMENTS = 8
CORES = 2


CONTRACT_FIRST = (((0,), (1,)), ((), ()))
CONTRACT_LAST = (((1,), (1,)), ((), ()))
DOM = ("zx", "core")
LANES = 128


def to_tiles(rows):
    lead = rows.shape[:-2]
    count, width = rows.shape[-2:]
    tiled = rows.reshape(lead + (count, width // LANES, LANES))
    return jnp.moveaxis(tiled, -2, -3)


def from_tiles(tiles):
    lead = tiles.shape[:-3]
    groups, count, lanes = tiles.shape[-3:]
    return jnp.moveaxis(tiles, -3, -2).reshape(lead + (count, groups * lanes))


def share_slots(slots, chips):
    swap = [(0, 1), (1, 0)]
    slots = slots + lax.ppermute(slots, "core", swap)
    core = lax.axis_index("core")
    count = slots.shape[0]
    halves = slots.reshape((CORES, count // CORES) + slots.shape[1:])
    mine = lax.dynamic_index_in_dim(halves, core, 0, keepdims=False)
    tile_shape = mine.shape[2:]
    pieces = lax.all_to_all(mine.reshape((chips,) + tile_shape), "zx", 0, 0, tiled=True)
    total = jnp.sum(pieces, axis=0, keepdims=True)
    spread = jnp.broadcast_to(total, (chips,) + tile_shape)
    gathered = lax.all_to_all(spread, "zx", 0, 0, tiled=True).reshape(mine.shape)
    other = lax.ppermute(gathered, "core", swap)
    return jnp.where(
        core == 0,
        jnp.concatenate([gathered, other]),
        jnp.concatenate([other, gathered]),
    )


def gather_rows(rows, subs):
    copies = jnp.broadcast_to(rows[None], (subs,) + rows.shape)
    pieces = lax.all_to_all(copies, "sub", 0, 0, tiled=True)
    return pieces.reshape((subs * rows.shape[0],) + rows.shape[1:])


def local(
    excitation,
    local_inverse,
    aggregation,
    disaggregation,
    translation,
    partners,
    list_counts,
    sweep_order,
):
    chips = lax.axis_size("zx")
    excite_rows = excitation[0]
    inverse_rows = local_inverse[0]
    agg_columns = aggregation[0]
    disagg_rows = disaggregation[0]
    trans_rows = translation[0]
    partner_row = partners[0]

    def apply_inverse(shard_rows):
        return jnp.dot(inverse_rows, shard_rows, preferred_element_type=jnp.float32)

    subs = lax.axis_size("sub")
    solved = apply_inverse(gather_rows(excite_rows, subs))
    solved_half = solved.astype(jnp.bfloat16)
    partial_incident = lax.dot_general(
        solved_half, agg_columns, CONTRACT_FIRST, preferred_element_type=jnp.float32
    ).astype(jnp.bfloat16)
    incident_pieces = lax.all_to_all(
        partial_incident.reshape((subs, -1) + partial_incident.shape[1:]), "sub", 0, 0, tiled=True
    )
    incident = jnp.sum(incident_pieces.astype(jnp.float32), axis=0)
    spread = apply_inverse(lax.all_gather(disagg_rows, "sub", axis=0, tiled=True))
    spread_half = spread.astype(jnp.bfloat16)
    partial_map = lax.dot_general(
        spread_half, agg_columns, CONTRACT_FIRST, preferred_element_type=jnp.float32
    ).astype(jnp.bfloat16)
    coupling = lax.psum(partial_map, "sub")

    domains = sweep_order.shape[0]
    members = domains // SEGMENTS
    segment_of = sweep_order * SEGMENTS // domains
    own_index = lax.axis_index("zx") * CORES + lax.axis_index("core")
    my_segment = segment_of[own_index]
    my_slot = sweep_order[own_index] - my_segment * members
    slot_ids = jnp.arange(members, dtype=jnp.int32)
    slot_live = jnp.arange(partner_row.shape[0], dtype=jnp.int32) < list_counts[0]
    partner_pos = sweep_order[partner_row]
    partner_segment = partner_pos * SEGMENTS // domains
    partner_slot = partner_pos - partner_segment * members

    half_samples = trans_rows.shape[-1] // LANES
    trans_tiles = trans_rows.reshape(trans_rows.shape[:2] + (half_samples, 1, LANES))
    incoming = jnp.zeros(to_tiles(incident).shape, jnp.float32)
    for segment_k in range(SEGMENTS - 1):
        if segment_k == 0:
            pattern = incident.astype(jnp.bfloat16)
        elif segment_k == 1:
            all_fields = gather_rows(from_tiles(incoming).astype(jnp.bfloat16), subs)
            products = jnp.dot(all_fields, partial_map, preferred_element_type=jnp.float32)
            product_pieces = lax.all_to_all(
                products.reshape((subs, -1) + products.shape[1:]), "sub", 0, 0, tiled=True
            )
            pattern = (incident - jnp.sum(product_pieces, axis=0)).astype(jnp.bfloat16)
        else:
            pattern = (
                incident
                - jnp.dot(
                    from_tiles(incoming).astype(jnp.bfloat16),
                    coupling,
                    preferred_element_type=jnp.float32,
                )
            ).astype(jnp.bfloat16)
        mine = (slot_ids == my_slot) & (my_segment == segment_k)
        pattern_tiles = to_tiles(pattern)
        slots = jnp.where(
            mine[:, None, None, None], pattern_tiles[None], jnp.zeros_like(pattern_tiles)[None]
        )
        slots = share_slots(slots, chips).astype(jnp.float32)
        match = (
            (partner_slot[:, None] == slot_ids[None, :])
            & (partner_segment[:, None] == segment_k)
            & slot_live[:, None]
            & (segment_k < my_segment)
        )
        weights = jnp.sum(
            jnp.where(match[:, :, None, None, None, None], trans_tiles[:, None], 0.0), axis=0
        )
        real_weight = weights[:, 0]
        imag_weight = weights[:, 1]
        real_part = slots[:, :half_samples]
        imag_part = slots[:, half_samples:]
        incoming = incoming + jnp.concatenate(
            [
                jnp.sum(real_weight * real_part - imag_weight * imag_part, axis=0),
                jnp.sum(real_weight * imag_part + imag_weight * real_part, axis=0),
            ],
            axis=0,
        )
    incoming = from_tiles(incoming)
    fields = gather_rows(incoming.astype(jnp.bfloat16), subs)
    currents = solved - lax.dot_general(
        spread_half, fields, CONTRACT_LAST, preferred_element_type=jnp.float32
    )
    return currents[None]


def solution(mesh):
    dom_size, sub_size = mesh.devices.shape
    fine = Mesh(mesh.devices.reshape(dom_size // CORES, CORES, sub_size), ("zx", "core", "sub"))
    in_specs = (
        P(DOM, "sub", None),
        P(DOM, "sub", None),
        P(DOM, None, "sub"),
        P(DOM, "sub", None),
        P(DOM, None, None, None),
        P(DOM, None),
        P(DOM),
        P(),
    )
    out_specs = P(DOM, "sub", None)
    return jax.shard_map(local, mesh=fine, in_specs=in_specs, out_specs=out_specs, check_vma=False)
```

```python
import jax
import jax.numpy as jnp
from jax import lax
from jax.sharding import Mesh
from jax.sharding import PartitionSpec as P

SEGMENTS = 8
CORES = 2


CONTRACT_FIRST = (((0,), (1,)), ((), ()))
CONTRACT_LAST = (((1,), (1,)), ((), ()))
DOM = ("zx", "core")
LANES = 128
PARTIAL_ROUNDS = 3


def to_tiles(rows):
    lead = rows.shape[:-2]
    count, width = rows.shape[-2:]
    tiled = rows.reshape(lead + (count, width // LANES, LANES))
    return jnp.moveaxis(tiled, -2, -3)


def from_tiles(tiles):
    lead = tiles.shape[:-3]
    groups, count, lanes = tiles.shape[-3:]
    return jnp.moveaxis(tiles, -3, -2).reshape(lead + (count, groups * lanes))


def share_slots(slots, chips):
    swap = [(0, 1), (1, 0)]
    slots = slots + lax.ppermute(slots, "core", swap)
    core = lax.axis_index("core")
    count = slots.shape[0]
    halves = slots.reshape((CORES, count // CORES) + slots.shape[1:])
    mine = lax.dynamic_index_in_dim(halves, core, 0, keepdims=False)
    tile_shape = mine.shape[2:]
    pieces = lax.all_to_all(mine.reshape((chips,) + tile_shape), "zx", 0, 0, tiled=True)
    total = jnp.sum(pieces, axis=0, keepdims=True)
    spread = jnp.broadcast_to(total, (chips,) + tile_shape)
    gathered = lax.all_to_all(spread, "zx", 0, 0, tiled=True).reshape(mine.shape)
    other = lax.ppermute(gathered, "core", swap)
    return jnp.where(
        core == 0,
        jnp.concatenate([gathered, other]),
        jnp.concatenate([other, gathered]),
    )


def gather_rows(rows, subs):
    copies = jnp.broadcast_to(rows[None], (subs,) + rows.shape)
    pieces = lax.all_to_all(copies, "sub", 0, 0, tiled=True)
    return pieces.reshape((subs * rows.shape[0],) + rows.shape[1:])


def local(
    excitation,
    local_inverse,
    aggregation,
    disaggregation,
    translation,
    partners,
    list_counts,
    sweep_order,
):
    chips = lax.axis_size("zx")
    excite_rows = excitation[0]
    inverse_rows = local_inverse[0]
    agg_columns = aggregation[0]
    disagg_rows = disaggregation[0]
    trans_rows = translation[0]
    partner_row = partners[0]

    def apply_inverse(shard_rows):
        return jnp.dot(inverse_rows, shard_rows, preferred_element_type=jnp.float32)

    subs = lax.axis_size("sub")
    solved = apply_inverse(gather_rows(excite_rows, subs))
    solved_half = solved.astype(jnp.bfloat16)
    partial_incident = lax.dot_general(
        solved_half, agg_columns, CONTRACT_FIRST, preferred_element_type=jnp.float32
    ).astype(jnp.bfloat16)
    incident_pieces = lax.all_to_all(
        partial_incident.reshape((subs, -1) + partial_incident.shape[1:]), "sub", 0, 0, tiled=True
    )
    incident = jnp.sum(incident_pieces.astype(jnp.float32), axis=0)
    spread = apply_inverse(lax.all_gather(disagg_rows, "sub", axis=0, tiled=True))
    spread_half = spread.astype(jnp.bfloat16)
    partial_map = lax.dot_general(
        spread_half, agg_columns, CONTRACT_FIRST, preferred_element_type=jnp.float32
    ).astype(jnp.bfloat16)
    coupling = lax.psum(partial_map, "sub")

    domains = sweep_order.shape[0]
    members = domains // SEGMENTS
    segment_of = sweep_order * SEGMENTS // domains
    own_index = lax.axis_index("zx") * CORES + lax.axis_index("core")
    my_segment = segment_of[own_index]
    my_slot = sweep_order[own_index] - my_segment * members
    slot_ids = jnp.arange(members, dtype=jnp.int32)
    slot_live = jnp.arange(partner_row.shape[0], dtype=jnp.int32) < list_counts[0]
    partner_pos = sweep_order[partner_row]
    partner_segment = partner_pos * SEGMENTS // domains
    partner_slot = partner_pos - partner_segment * members

    half_samples = trans_rows.shape[-1] // LANES
    trans_tiles = trans_rows.reshape(trans_rows.shape[:2] + (half_samples, 1, LANES))
    incoming = jnp.zeros(to_tiles(incident).shape, jnp.float32)
    for segment_k in range(SEGMENTS - 1):
        if segment_k == 0:
            pattern = incident.astype(jnp.bfloat16)
        elif segment_k < PARTIAL_ROUNDS:
            all_fields = gather_rows(from_tiles(incoming).astype(jnp.bfloat16), subs)
            products = jnp.dot(all_fields, partial_map, preferred_element_type=jnp.float32)
            product_pieces = lax.all_to_all(
                products.reshape((subs, -1) + products.shape[1:]), "sub", 0, 0, tiled=True
            )
            pattern = (incident - jnp.sum(product_pieces, axis=0)).astype(jnp.bfloat16)
        else:
            pattern = (
                incident
                - jnp.dot(
                    from_tiles(incoming).astype(jnp.bfloat16),
                    coupling,
                    preferred_element_type=jnp.float32,
                )
            ).astype(jnp.bfloat16)
        mine = (slot_ids == my_slot) & (my_segment == segment_k)
        pattern_tiles = to_tiles(pattern)
        slots = jnp.where(
            mine[:, None, None, None], pattern_tiles[None], jnp.zeros_like(pattern_tiles)[None]
        )
        slots = share_slots(slots, chips).astype(jnp.float32)
        match = (
            (partner_slot[:, None] == slot_ids[None, :])
            & (partner_segment[:, None] == segment_k)
            & slot_live[:, None]
            & (segment_k < my_segment)
        )
        weights = jnp.sum(
            jnp.where(match[:, :, None, None, None, None], trans_tiles[:, None], 0.0), axis=0
        )
        real_weight = weights[:, 0]
        imag_weight = weights[:, 1]
        real_part = slots[:, :half_samples]
        imag_part = slots[:, half_samples:]
        incoming = incoming + jnp.concatenate(
            [
                jnp.sum(real_weight * real_part - imag_weight * imag_part, axis=0),
                jnp.sum(real_weight * imag_part + imag_weight * real_part, axis=0),
            ],
            axis=0,
        )
    incoming = from_tiles(incoming)
    fields = gather_rows(incoming.astype(jnp.bfloat16), subs)
    currents = solved - lax.dot_general(
        spread_half, fields, CONTRACT_LAST, preferred_element_type=jnp.float32
    )
    return currents[None]


def solution(mesh):
    dom_size, sub_size = mesh.devices.shape
    fine = Mesh(mesh.devices.reshape(dom_size // CORES, CORES, sub_size), ("zx", "core", "sub"))
    in_specs = (
        P(DOM, "sub", None),
        P(DOM, "sub", None),
        P(DOM, None, "sub"),
        P(DOM, "sub", None),
        P(DOM, None, None, None),
        P(DOM, None),
        P(DOM),
        P(),
    )
    out_specs = P(DOM, "sub", None)
    return jax.shard_map(local, mesh=fine, in_specs=in_specs, out_specs=out_specs, check_vma=False)
```

```python
import jax
import jax.numpy as jnp
from jax import lax
from jax.sharding import Mesh
from jax.sharding import PartitionSpec as P

SEGMENTS = 8
CORES = 2


CONTRACT_FIRST = (((0,), (1,)), ((), ()))
CONTRACT_LAST = (((1,), (1,)), ((), ()))
DOM = ("zx", "core")
LANES = 128


def to_tiles(rows):
    lead = rows.shape[:-2]
    count, width = rows.shape[-2:]
    tiled = rows.reshape(lead + (count, width // LANES, LANES))
    return jnp.moveaxis(tiled, -2, -3)


def from_tiles(tiles):
    lead = tiles.shape[:-3]
    groups, count, lanes = tiles.shape[-3:]
    return jnp.moveaxis(tiles, -3, -2).reshape(lead + (count, groups * lanes))


def share_slots(slots, chips):
    swap = [(0, 1), (1, 0)]
    slots = slots + lax.ppermute(slots, "core", swap)
    core = lax.axis_index("core")
    count = slots.shape[0]
    halves = slots.reshape((CORES, count // CORES) + slots.shape[1:])
    mine = lax.dynamic_index_in_dim(halves, core, 0, keepdims=False)
    tile_shape = mine.shape[2:]
    pieces = lax.all_to_all(mine.reshape((chips,) + tile_shape), "zx", 0, 0, tiled=True)
    total = jnp.sum(pieces, axis=0, keepdims=True)
    spread = jnp.broadcast_to(total, (chips,) + tile_shape)
    gathered = lax.all_to_all(spread, "zx", 0, 0, tiled=True).reshape(mine.shape)
    other = lax.ppermute(gathered, "core", swap)
    return jnp.where(
        core == 0,
        jnp.concatenate([gathered, other]),
        jnp.concatenate([other, gathered]),
    )


def from_partners(value_for, subs):
    received = [value_for(0)]
    for hop in range(1, subs):
        received.append(lax.ppermute(value_for(hop), "sub", [(i, i ^ hop) for i in range(subs)]))
    return jnp.stack(received)


def gather_rows(rows, subs):
    received = from_partners(lambda hop: rows, subs)
    order = lax.axis_index("sub") ^ jnp.arange(subs, dtype=jnp.int32)
    return received[order].reshape((subs * rows.shape[0],) + rows.shape[1:])


def broadcast_rows(rows, subs):
    copies = jnp.broadcast_to(rows[None], (subs,) + rows.shape)
    pieces = lax.all_to_all(copies, "sub", 0, 0, tiled=True)
    return pieces.reshape((subs * rows.shape[0],) + rows.shape[1:])


def scatter_sum(blocks, subs):
    own = lax.axis_index("sub")
    received = from_partners(
        lambda hop: lax.dynamic_index_in_dim(blocks, own ^ hop, 0, keepdims=False), subs
    )
    return jnp.sum(received.astype(jnp.float32), axis=0)


def local(
    excitation,
    local_inverse,
    aggregation,
    disaggregation,
    translation,
    partners,
    list_counts,
    sweep_order,
):
    chips = lax.axis_size("zx")
    excite_rows = excitation[0]
    inverse_rows = local_inverse[0]
    agg_columns = aggregation[0]
    disagg_rows = disaggregation[0]
    trans_rows = translation[0]
    partner_row = partners[0]

    def apply_inverse(shard_rows):
        return jnp.dot(inverse_rows, shard_rows, preferred_element_type=jnp.float32)

    subs = lax.axis_size("sub")
    solved = apply_inverse(broadcast_rows(excite_rows, subs))
    solved_half = solved.astype(jnp.bfloat16)
    partial_incident = lax.dot_general(
        solved_half, agg_columns, CONTRACT_FIRST, preferred_element_type=jnp.float32
    ).astype(jnp.bfloat16)
    incident = scatter_sum(partial_incident.reshape((subs, -1) + partial_incident.shape[1:]), subs)
    spread = apply_inverse(lax.all_gather(disagg_rows, "sub", axis=0, tiled=True))
    spread_half = spread.astype(jnp.bfloat16)
    partial_map = lax.dot_general(
        spread_half, agg_columns, CONTRACT_FIRST, preferred_element_type=jnp.float32
    ).astype(jnp.bfloat16)
    coupling = lax.psum(partial_map, "sub")

    domains = sweep_order.shape[0]
    members = domains // SEGMENTS
    segment_of = sweep_order * SEGMENTS // domains
    own_index = lax.axis_index("zx") * CORES + lax.axis_index("core")
    my_segment = segment_of[own_index]
    my_slot = sweep_order[own_index] - my_segment * members
    slot_ids = jnp.arange(members, dtype=jnp.int32)
    slot_live = jnp.arange(partner_row.shape[0], dtype=jnp.int32) < list_counts[0]
    partner_pos = sweep_order[partner_row]
    partner_segment = partner_pos * SEGMENTS // domains
    partner_slot = partner_pos - partner_segment * members

    half_samples = trans_rows.shape[-1] // LANES
    trans_tiles = trans_rows.reshape(trans_rows.shape[:2] + (half_samples, 1, LANES))
    incoming = jnp.zeros(to_tiles(incident).shape, jnp.float32)
    for segment_k in range(SEGMENTS - 1):
        if segment_k == 0:
            pattern = incident.astype(jnp.bfloat16)
        elif segment_k == 1:
            all_fields = gather_rows(from_tiles(incoming).astype(jnp.bfloat16), subs)
            products = jnp.dot(all_fields, partial_map, preferred_element_type=jnp.float32)
            coupled = scatter_sum(products.reshape((subs, -1) + products.shape[1:]), subs)
            pattern = (incident - coupled).astype(jnp.bfloat16)
        else:
            pattern = (
                incident
                - jnp.dot(
                    from_tiles(incoming).astype(jnp.bfloat16),
                    coupling,
                    preferred_element_type=jnp.float32,
                )
            ).astype(jnp.bfloat16)
        mine = (slot_ids == my_slot) & (my_segment == segment_k)
        pattern_tiles = to_tiles(pattern)
        slots = jnp.where(
            mine[:, None, None, None], pattern_tiles[None], jnp.zeros_like(pattern_tiles)[None]
        )
        slots = share_slots(slots, chips).astype(jnp.float32)
        match = (
            (partner_slot[:, None] == slot_ids[None, :])
            & (partner_segment[:, None] == segment_k)
            & slot_live[:, None]
            & (segment_k < my_segment)
        )
        weights = jnp.sum(
            jnp.where(match[:, :, None, None, None, None], trans_tiles[:, None], 0.0), axis=0
        )
        real_weight = weights[:, 0]
        imag_weight = weights[:, 1]
        real_part = slots[:, :half_samples]
        imag_part = slots[:, half_samples:]
        incoming = incoming + jnp.concatenate(
            [
                jnp.sum(real_weight * real_part - imag_weight * imag_part, axis=0),
                jnp.sum(real_weight * imag_part + imag_weight * real_part, axis=0),
            ],
            axis=0,
        )
    incoming = from_tiles(incoming)
    fields = gather_rows(incoming.astype(jnp.bfloat16), subs)
    currents = solved - lax.dot_general(
        spread_half, fields, CONTRACT_LAST, preferred_element_type=jnp.float32
    )
    return currents[None]


def solution(mesh):
    dom_size, sub_size = mesh.devices.shape
    fine = Mesh(mesh.devices.reshape(dom_size // CORES, CORES, sub_size), ("zx", "core", "sub"))
    in_specs = (
        P(DOM, "sub", None),
        P(DOM, "sub", None),
        P(DOM, None, "sub"),
        P(DOM, "sub", None),
        P(DOM, None, None, None),
        P(DOM, None),
        P(DOM),
        P(),
    )
    out_specs = P(DOM, "sub", None)
    return jax.shard_map(local, mesh=fine, in_specs=in_specs, out_specs=out_specs, check_vma=False)
```

```python
import jax
import jax.numpy as jnp
from jax import lax
from jax.sharding import Mesh
from jax.sharding import PartitionSpec as P

SEGMENTS = 8
CORES = 2


CONTRACT_FIRST = (((0,), (1,)), ((), ()))
CONTRACT_LAST = (((1,), (1,)), ((), ()))
DOM = ("zx", "core")
LANES = 128


def to_tiles(rows):
    lead = rows.shape[:-2]
    count, width = rows.shape[-2:]
    tiled = rows.reshape(lead + (count, width // LANES, LANES))
    return jnp.moveaxis(tiled, -2, -3)


def from_tiles(tiles):
    lead = tiles.shape[:-3]
    groups, count, lanes = tiles.shape[-3:]
    return jnp.moveaxis(tiles, -3, -2).reshape(lead + (count, groups * lanes))


def share_slots(slots, chips):
    swap = [(0, 1), (1, 0)]
    slots = slots + lax.ppermute(slots, "core", swap)
    core = lax.axis_index("core")
    count = slots.shape[0]
    halves = slots.reshape((CORES, count // CORES) + slots.shape[1:])
    mine = lax.dynamic_index_in_dim(halves, core, 0, keepdims=False)
    tile_shape = mine.shape[2:]
    pieces = lax.all_to_all(mine.reshape((chips,) + tile_shape), "zx", 0, 0, tiled=True)
    total = jnp.sum(pieces, axis=0, keepdims=True)
    spread = jnp.broadcast_to(total, (chips,) + tile_shape)
    gathered = lax.all_to_all(spread, "zx", 0, 0, tiled=True).reshape(mine.shape)
    other = lax.ppermute(gathered, "core", swap)
    return jnp.where(
        core == 0,
        jnp.concatenate([gathered, other]),
        jnp.concatenate([other, gathered]),
    )


def from_partners(value_for, subs):
    received = [value_for(0)]
    for hop in range(1, subs):
        received.append(lax.ppermute(value_for(hop), "sub", [(i, i ^ hop) for i in range(subs)]))
    return jnp.stack(received)


def gather_rows(rows, subs):
    received = from_partners(lambda hop: rows, subs)
    order = lax.axis_index("sub") ^ jnp.arange(subs, dtype=jnp.int32)
    return received[order].reshape((subs * rows.shape[0],) + rows.shape[1:])


def broadcast_rows(rows, subs):
    copies = jnp.broadcast_to(rows[None], (subs,) + rows.shape)
    pieces = lax.all_to_all(copies, "sub", 0, 0, tiled=True)
    return pieces.reshape((subs * rows.shape[0],) + rows.shape[1:])


def scatter_sum(blocks, subs):
    own = lax.axis_index("sub")
    received = from_partners(
        lambda hop: lax.dynamic_index_in_dim(blocks, own ^ hop, 0, keepdims=False), subs
    )
    return jnp.sum(received.astype(jnp.float32), axis=0)


def local(
    excitation,
    local_inverse,
    aggregation,
    disaggregation,
    translation,
    partners,
    list_counts,
    sweep_order,
):
    chips = lax.axis_size("zx")
    excite_rows = excitation[0]
    inverse_rows = local_inverse[0]
    agg_columns = aggregation[0]
    disagg_rows = disaggregation[0]
    trans_rows = translation[0]
    partner_row = partners[0]

    def apply_inverse(shard_rows):
        return jnp.dot(inverse_rows, shard_rows, preferred_element_type=jnp.float32)

    subs = lax.axis_size("sub")
    solved = apply_inverse(broadcast_rows(excite_rows, subs))
    solved_half = solved.astype(jnp.bfloat16)
    partial_incident = lax.dot_general(
        solved_half, agg_columns, CONTRACT_FIRST, preferred_element_type=jnp.float32
    ).astype(jnp.bfloat16)
    incident = scatter_sum(partial_incident.reshape((subs, -1) + partial_incident.shape[1:]), subs)
    sub_index = lax.axis_index("sub")
    block = disagg_rows.shape[0]
    disagg_parts = from_partners(lambda hop: disagg_rows, subs)
    spread = jnp.zeros((inverse_rows.shape[0], disagg_rows.shape[1]), jnp.float32)
    for hop in range(subs):
        columns = lax.dynamic_slice_in_dim(inverse_rows, (sub_index ^ hop) * block, block, axis=1)
        spread = spread + jnp.dot(columns, disagg_parts[hop], preferred_element_type=jnp.float32)
    spread_half = spread.astype(jnp.bfloat16)
    partial_map = lax.dot_general(
        spread_half, agg_columns, CONTRACT_FIRST, preferred_element_type=jnp.float32
    ).astype(jnp.bfloat16)
    map_share = scatter_sum(partial_map.reshape((subs, -1) + partial_map.shape[1:]), subs)
    coupling = gather_rows(map_share.astype(jnp.bfloat16), subs)

    domains = sweep_order.shape[0]
    members = domains // SEGMENTS
    segment_of = sweep_order * SEGMENTS // domains
    own_index = lax.axis_index("zx") * CORES + lax.axis_index("core")
    my_segment = segment_of[own_index]
    my_slot = sweep_order[own_index] - my_segment * members
    slot_ids = jnp.arange(members, dtype=jnp.int32)
    slot_live = jnp.arange(partner_row.shape[0], dtype=jnp.int32) < list_counts[0]
    partner_pos = sweep_order[partner_row]
    partner_segment = partner_pos * SEGMENTS // domains
    partner_slot = partner_pos - partner_segment * members

    half_samples = trans_rows.shape[-1] // LANES
    trans_tiles = trans_rows.reshape(trans_rows.shape[:2] + (half_samples, 1, LANES))
    incoming = jnp.zeros(to_tiles(incident).shape, jnp.float32)
    for segment_k in range(SEGMENTS - 1):
        if segment_k == 0:
            pattern = incident.astype(jnp.bfloat16)
        elif segment_k == 1:
            all_fields = gather_rows(from_tiles(incoming).astype(jnp.bfloat16), subs)
            products = jnp.dot(all_fields, partial_map, preferred_element_type=jnp.float32)
            coupled = scatter_sum(products.reshape((subs, -1) + products.shape[1:]), subs)
            pattern = (incident - coupled).astype(jnp.bfloat16)
        else:
            pattern = (
                incident
                - jnp.dot(
                    from_tiles(incoming).astype(jnp.bfloat16),
                    coupling,
                    preferred_element_type=jnp.float32,
                )
            ).astype(jnp.bfloat16)
        mine = (slot_ids == my_slot) & (my_segment == segment_k)
        pattern_tiles = to_tiles(pattern)
        slots = jnp.where(
            mine[:, None, None, None], pattern_tiles[None], jnp.zeros_like(pattern_tiles)[None]
        )
        slots = share_slots(slots, chips).astype(jnp.float32)
        match = (
            (partner_slot[:, None] == slot_ids[None, :])
            & (partner_segment[:, None] == segment_k)
            & slot_live[:, None]
            & (segment_k < my_segment)
        )
        weights = jnp.sum(
            jnp.where(match[:, :, None, None, None, None], trans_tiles[:, None], 0.0), axis=0
        )
        real_weight = weights[:, 0]
        imag_weight = weights[:, 1]
        real_part = slots[:, :half_samples]
        imag_part = slots[:, half_samples:]
        incoming = incoming + jnp.concatenate(
            [
                jnp.sum(real_weight * real_part - imag_weight * imag_part, axis=0),
                jnp.sum(real_weight * imag_part + imag_weight * real_part, axis=0),
            ],
            axis=0,
        )
    incoming = from_tiles(incoming)
    fields = gather_rows(incoming.astype(jnp.bfloat16), subs)
    currents = solved - lax.dot_general(
        spread_half, fields, CONTRACT_LAST, preferred_element_type=jnp.float32
    )
    return currents[None]


def solution(mesh):
    dom_size, sub_size = mesh.devices.shape
    fine = Mesh(mesh.devices.reshape(dom_size // CORES, CORES, sub_size), ("zx", "core", "sub"))
    in_specs = (
        P(DOM, "sub", None),
        P(DOM, "sub", None),
        P(DOM, None, "sub"),
        P(DOM, "sub", None),
        P(DOM, None, None, None),
        P(DOM, None),
        P(DOM),
        P(),
    )
    out_specs = P(DOM, "sub", None)
    return jax.shard_map(local, mesh=fine, in_specs=in_specs, out_specs=out_specs, check_vma=False)
```

```python
import jax
import jax.numpy as jnp
from jax import lax
from jax.sharding import Mesh
from jax.sharding import PartitionSpec as P

SEGMENTS = 8
CORES = 2


CONTRACT_FIRST = (((0,), (1,)), ((), ()))
CONTRACT_LAST = (((1,), (1,)), ((), ()))
DOM = ("zx", "core")
LANES = 128


def to_tiles(rows):
    lead = rows.shape[:-2]
    count, width = rows.shape[-2:]
    tiled = rows.reshape(lead + (count, width // LANES, LANES))
    return jnp.moveaxis(tiled, -2, -3)


def from_tiles(tiles):
    lead = tiles.shape[:-3]
    groups, count, lanes = tiles.shape[-3:]
    return jnp.moveaxis(tiles, -3, -2).reshape(lead + (count, groups * lanes))


def share_slots(slots, chips):
    swap = [(0, 1), (1, 0)]
    core = lax.axis_index("core")
    count = slots.shape[0]
    halves = slots.reshape((CORES, count // CORES) + slots.shape[1:])
    wanted = lax.dynamic_index_in_dim(halves, 1 - core, 0, keepdims=False)
    mine = lax.dynamic_index_in_dim(halves, core, 0, keepdims=False)
    mine = mine + lax.ppermute(wanted, "core", swap)
    tile_shape = mine.shape[2:]
    pieces = lax.all_to_all(mine.reshape((chips,) + tile_shape), "zx", 0, 0, tiled=True)
    total = jnp.sum(pieces, axis=0, keepdims=True)
    spread = jnp.broadcast_to(total, (chips,) + tile_shape)
    gathered = lax.all_to_all(spread, "zx", 0, 0, tiled=True).reshape(mine.shape)
    other = lax.ppermute(gathered, "core", swap)
    return jnp.where(
        core == 0,
        jnp.concatenate([gathered, other]),
        jnp.concatenate([other, gathered]),
    )


def from_partners(value_for, subs):
    received = [value_for(0)]
    for hop in range(1, subs):
        received.append(lax.ppermute(value_for(hop), "sub", [(i, i ^ hop) for i in range(subs)]))
    return jnp.stack(received)


def gather_rows(rows, subs):
    received = from_partners(lambda hop: rows, subs)
    order = lax.axis_index("sub") ^ jnp.arange(subs, dtype=jnp.int32)
    return received[order].reshape((subs * rows.shape[0],) + rows.shape[1:])


def broadcast_rows(rows, subs):
    copies = jnp.broadcast_to(rows[None], (subs,) + rows.shape)
    pieces = lax.all_to_all(copies, "sub", 0, 0, tiled=True)
    return pieces.reshape((subs * rows.shape[0],) + rows.shape[1:])


def scatter_sum(blocks, subs):
    own = lax.axis_index("sub")
    received = from_partners(
        lambda hop: lax.dynamic_index_in_dim(blocks, own ^ hop, 0, keepdims=False), subs
    )
    return jnp.sum(received.astype(jnp.float32), axis=0)


def local(
    excitation,
    local_inverse,
    aggregation,
    disaggregation,
    translation,
    partners,
    list_counts,
    sweep_order,
):
    chips = lax.axis_size("zx")
    excite_rows = excitation[0]
    inverse_rows = local_inverse[0]
    agg_columns = aggregation[0]
    disagg_rows = disaggregation[0]
    trans_rows = translation[0]
    partner_row = partners[0]

    def apply_inverse(shard_rows):
        return jnp.dot(inverse_rows, shard_rows, preferred_element_type=jnp.float32)

    subs = lax.axis_size("sub")
    solved = apply_inverse(broadcast_rows(excite_rows, subs))
    solved_half = solved.astype(jnp.bfloat16)
    partial_incident = lax.dot_general(
        solved_half, agg_columns, CONTRACT_FIRST, preferred_element_type=jnp.float32
    ).astype(jnp.bfloat16)
    incident = scatter_sum(partial_incident.reshape((subs, -1) + partial_incident.shape[1:]), subs)
    spread = apply_inverse(lax.all_gather(disagg_rows, "sub", axis=0, tiled=True))
    spread_half = spread.astype(jnp.bfloat16)
    partial_map = lax.dot_general(
        spread_half, agg_columns, CONTRACT_FIRST, preferred_element_type=jnp.float32
    ).astype(jnp.bfloat16)
    coupling = lax.psum(partial_map, "sub")

    domains = sweep_order.shape[0]
    members = domains // SEGMENTS
    segment_of = sweep_order * SEGMENTS // domains
    own_index = lax.axis_index("zx") * CORES + lax.axis_index("core")
    my_segment = segment_of[own_index]
    my_slot = sweep_order[own_index] - my_segment * members
    slot_ids = jnp.arange(members, dtype=jnp.int32)
    slot_live = jnp.arange(partner_row.shape[0], dtype=jnp.int32) < list_counts[0]
    partner_pos = sweep_order[partner_row]
    partner_segment = partner_pos * SEGMENTS // domains
    partner_slot = partner_pos - partner_segment * members

    half_samples = trans_rows.shape[-1] // LANES
    trans_tiles = trans_rows.reshape(trans_rows.shape[:2] + (half_samples, 1, LANES))
    incoming = jnp.zeros(to_tiles(incident).shape, jnp.float32)
    for segment_k in range(SEGMENTS - 1):
        if segment_k == 0:
            pattern = incident.astype(jnp.bfloat16)
        elif segment_k == 1:
            all_fields = gather_rows(from_tiles(incoming).astype(jnp.bfloat16), subs)
            products = jnp.dot(all_fields, partial_map, preferred_element_type=jnp.float32)
            coupled = scatter_sum(products.reshape((subs, -1) + products.shape[1:]), subs)
            pattern = (incident - coupled).astype(jnp.bfloat16)
        else:
            pattern = (
                incident
                - jnp.dot(
                    from_tiles(incoming).astype(jnp.bfloat16),
                    coupling,
                    preferred_element_type=jnp.float32,
                )
            ).astype(jnp.bfloat16)
        mine = (slot_ids == my_slot) & (my_segment == segment_k)
        pattern_tiles = to_tiles(pattern)
        slots = jnp.where(
            mine[:, None, None, None], pattern_tiles[None], jnp.zeros_like(pattern_tiles)[None]
        )
        slots = share_slots(slots, chips).astype(jnp.float32)
        match = (
            (partner_slot[:, None] == slot_ids[None, :])
            & (partner_segment[:, None] == segment_k)
            & slot_live[:, None]
            & (segment_k < my_segment)
        )
        weights = jnp.sum(
            jnp.where(match[:, :, None, None, None, None], trans_tiles[:, None], 0.0), axis=0
        )
        real_weight = weights[:, 0]
        imag_weight = weights[:, 1]
        real_part = slots[:, :half_samples]
        imag_part = slots[:, half_samples:]
        incoming = incoming + jnp.concatenate(
            [
                jnp.sum(real_weight * real_part - imag_weight * imag_part, axis=0),
                jnp.sum(real_weight * imag_part + imag_weight * real_part, axis=0),
            ],
            axis=0,
        )
    incoming = from_tiles(incoming)
    fields = gather_rows(incoming.astype(jnp.bfloat16), subs)
    currents = solved - lax.dot_general(
        spread_half, fields, CONTRACT_LAST, preferred_element_type=jnp.float32
    )
    return currents[None]


def solution(mesh):
    dom_size, sub_size = mesh.devices.shape
    fine = Mesh(mesh.devices.reshape(dom_size // CORES, CORES, sub_size), ("zx", "core", "sub"))
    in_specs = (
        P(DOM, "sub", None),
        P(DOM, "sub", None),
        P(DOM, None, "sub"),
        P(DOM, "sub", None),
        P(DOM, None, None, None),
        P(DOM, None),
        P(DOM),
        P(),
    )
    out_specs = P(DOM, "sub", None)
    return jax.shard_map(local, mesh=fine, in_specs=in_specs, out_specs=out_specs, check_vma=False)
```

```python
import jax
import jax.numpy as jnp
from jax import lax
from jax.sharding import Mesh
from jax.sharding import PartitionSpec as P

SEGMENTS = 8
CORES = 2


CONTRACT_FIRST = (((0,), (1,)), ((), ()))
CONTRACT_LAST = (((1,), (1,)), ((), ()))
DOM = ("zx", "core")
LANES = 128


def to_tiles(rows):
    lead = rows.shape[:-2]
    count, width = rows.shape[-2:]
    tiled = rows.reshape(lead + (count, width // LANES, LANES))
    return jnp.moveaxis(tiled, -2, -3)


def from_tiles(tiles):
    lead = tiles.shape[:-3]
    groups, count, lanes = tiles.shape[-3:]
    return jnp.moveaxis(tiles, -3, -2).reshape(lead + (count, groups * lanes))


def share_slots(slots, chips):
    swap = [(0, 1), (1, 0)]
    core = lax.axis_index("core")
    count = slots.shape[0]
    halves = slots.reshape((CORES, count // CORES) + slots.shape[1:])
    wanted = lax.dynamic_index_in_dim(halves, 1 - core, 0, keepdims=False)
    mine = lax.dynamic_index_in_dim(halves, core, 0, keepdims=False)
    mine = mine + lax.ppermute(wanted, "core", swap)
    tile_shape = mine.shape[2:]
    pieces = lax.all_to_all(mine.reshape((chips,) + tile_shape), "zx", 0, 0, tiled=True)
    total = jnp.sum(pieces, axis=0, keepdims=True)
    spread = jnp.broadcast_to(total, (chips,) + tile_shape)
    gathered = lax.all_to_all(spread, "zx", 0, 0, tiled=True).reshape(mine.shape)
    other = lax.ppermute(gathered, "core", swap)
    return gathered, other


def from_partners(value_for, subs):
    received = [value_for(0)]
    for hop in range(1, subs):
        received.append(lax.ppermute(value_for(hop), "sub", [(i, i ^ hop) for i in range(subs)]))
    return jnp.stack(received)


def gather_rows(rows, subs):
    received = from_partners(lambda hop: rows, subs)
    order = lax.axis_index("sub") ^ jnp.arange(subs, dtype=jnp.int32)
    return received[order].reshape((subs * rows.shape[0],) + rows.shape[1:])


def broadcast_rows(rows, subs):
    copies = jnp.broadcast_to(rows[None], (subs,) + rows.shape)
    pieces = lax.all_to_all(copies, "sub", 0, 0, tiled=True)
    return pieces.reshape((subs * rows.shape[0],) + rows.shape[1:])


def scatter_sum(blocks, subs):
    own = lax.axis_index("sub")
    received = from_partners(
        lambda hop: lax.dynamic_index_in_dim(blocks, own ^ hop, 0, keepdims=False), subs
    )
    return jnp.sum(received.astype(jnp.float32), axis=0)


def local(
    excitation,
    local_inverse,
    aggregation,
    disaggregation,
    translation,
    partners,
    list_counts,
    sweep_order,
):
    chips = lax.axis_size("zx")
    excite_rows = excitation[0]
    inverse_rows = local_inverse[0]
    agg_columns = aggregation[0]
    disagg_rows = disaggregation[0]
    trans_rows = translation[0]
    partner_row = partners[0]

    def apply_inverse(shard_rows):
        return jnp.dot(inverse_rows, shard_rows, preferred_element_type=jnp.float32)

    subs = lax.axis_size("sub")
    solved = apply_inverse(broadcast_rows(excite_rows, subs))
    solved_half = solved.astype(jnp.bfloat16)
    partial_incident = lax.dot_general(
        solved_half, agg_columns, CONTRACT_FIRST, preferred_element_type=jnp.float32
    ).astype(jnp.bfloat16)
    incident = scatter_sum(partial_incident.reshape((subs, -1) + partial_incident.shape[1:]), subs)
    spread = apply_inverse(lax.all_gather(disagg_rows, "sub", axis=0, tiled=True))
    spread_half = spread.astype(jnp.bfloat16)
    partial_map = lax.dot_general(
        spread_half, agg_columns, CONTRACT_FIRST, preferred_element_type=jnp.float32
    ).astype(jnp.bfloat16)
    coupling = lax.psum(partial_map, "sub")

    domains = sweep_order.shape[0]
    members = domains // SEGMENTS
    segment_of = sweep_order * SEGMENTS // domains
    own_index = lax.axis_index("zx") * CORES + lax.axis_index("core")
    my_segment = segment_of[own_index]
    my_slot = sweep_order[own_index] - my_segment * members
    slot_ids = jnp.arange(members, dtype=jnp.int32)
    slot_live = jnp.arange(partner_row.shape[0], dtype=jnp.int32) < list_counts[0]
    partner_pos = sweep_order[partner_row]
    partner_segment = partner_pos * SEGMENTS // domains
    partner_slot = partner_pos - partner_segment * members

    half_samples = trans_rows.shape[-1] // LANES
    trans_tiles = trans_rows.reshape(trans_rows.shape[:2] + (half_samples, 1, LANES))
    incoming = jnp.zeros(to_tiles(incident).shape, jnp.float32)
    for segment_k in range(SEGMENTS - 1):
        if segment_k == 0:
            pattern = incident.astype(jnp.bfloat16)
        elif segment_k == 1:
            all_fields = broadcast_rows(from_tiles(incoming).astype(jnp.bfloat16), subs)
            products = jnp.dot(all_fields, partial_map, preferred_element_type=jnp.float32)
            coupled = scatter_sum(products.reshape((subs, -1) + products.shape[1:]), subs)
            pattern = (incident - coupled).astype(jnp.bfloat16)
        else:
            pattern = (
                incident
                - jnp.dot(
                    from_tiles(incoming).astype(jnp.bfloat16),
                    coupling,
                    preferred_element_type=jnp.float32,
                )
            ).astype(jnp.bfloat16)
        mine = (slot_ids == my_slot) & (my_segment == segment_k)
        pattern_tiles = to_tiles(pattern)
        slots = jnp.where(
            mine[:, None, None, None], pattern_tiles[None], jnp.zeros_like(pattern_tiles)[None]
        )
        gathered, other = share_slots(slots, chips)
        match = (
            (partner_slot[:, None] == slot_ids[None, :])
            & (partner_segment[:, None] == segment_k)
            & slot_live[:, None]
            & (segment_k < my_segment)
        )
        weights = jnp.sum(
            jnp.where(match[:, :, None, None, None, None], trans_tiles[:, None], 0.0), axis=0
        )
        weight_halves = weights.reshape((CORES, members // CORES) + weights.shape[1:])
        core = lax.axis_index("core")
        ordered_weights = jnp.concatenate(
            [
                lax.dynamic_index_in_dim(weight_halves, core, 0, keepdims=False),
                lax.dynamic_index_in_dim(weight_halves, 1 - core, 0, keepdims=False),
            ]
        )
        values = jnp.concatenate([gathered, other]).astype(jnp.float32)
        real_weight = ordered_weights[:, 0]
        imag_weight = ordered_weights[:, 1]
        real_part = values[:, :half_samples]
        imag_part = values[:, half_samples:]
        incoming = incoming + jnp.concatenate(
            [
                jnp.sum(real_weight * real_part - imag_weight * imag_part, axis=0),
                jnp.sum(real_weight * imag_part + imag_weight * real_part, axis=0),
            ],
            axis=0,
        )
    incoming = from_tiles(incoming)
    fields = gather_rows(incoming.astype(jnp.bfloat16), subs)
    currents = solved - lax.dot_general(
        spread_half, fields, CONTRACT_LAST, preferred_element_type=jnp.float32
    )
    return currents[None]


def solution(mesh):
    dom_size, sub_size = mesh.devices.shape
    fine = Mesh(mesh.devices.reshape(dom_size // CORES, CORES, sub_size), ("zx", "core", "sub"))
    in_specs = (
        P(DOM, "sub", None),
        P(DOM, "sub", None),
        P(DOM, None, "sub"),
        P(DOM, "sub", None),
        P(DOM, None, None, None),
        P(DOM, None),
        P(DOM),
        P(),
    )
    out_specs = P(DOM, "sub", None)
    return jax.shard_map(local, mesh=fine, in_specs=in_specs, out_specs=out_specs, check_vma=False)
```

```python
import jax
import jax.numpy as jnp
from jax import lax
from jax.sharding import Mesh
from jax.sharding import PartitionSpec as P

SEGMENTS = 8
CORES = 2


CONTRACT_FIRST = (((0,), (1,)), ((), ()))
CONTRACT_LAST = (((1,), (1,)), ((), ()))
DOM = ("zx", "core")
LANES = 128


def to_tiles(rows):
    lead = rows.shape[:-2]
    count, width = rows.shape[-2:]
    tiled = rows.reshape(lead + (count, width // LANES, LANES))
    return jnp.moveaxis(tiled, -2, -3)


def from_tiles(tiles):
    lead = tiles.shape[:-3]
    groups, count, lanes = tiles.shape[-3:]
    return jnp.moveaxis(tiles, -3, -2).reshape(lead + (count, groups * lanes))


def share_slots(slots, chips):
    swap = [(0, 1), (1, 0)]
    core = lax.axis_index("core")
    count = slots.shape[0]
    halves = slots.reshape((CORES, count // CORES) + slots.shape[1:])
    wanted = lax.dynamic_index_in_dim(halves, 1 - core, 0, keepdims=False)
    mine = lax.dynamic_index_in_dim(halves, core, 0, keepdims=False)
    mine = mine + lax.ppermute(wanted, "core", swap)
    tile_shape = mine.shape[2:]
    pieces = lax.all_to_all(mine.reshape((chips,) + tile_shape), "zx", 0, 0, tiled=True)
    total = jnp.sum(pieces, axis=0, keepdims=True)
    spread = jnp.broadcast_to(total, (chips,) + tile_shape)
    gathered = lax.all_to_all(spread, "zx", 0, 0, tiled=True).reshape(mine.shape)
    other = lax.ppermute(gathered, "core", swap)
    return jnp.where(
        core == 0,
        jnp.concatenate([gathered, other]),
        jnp.concatenate([other, gathered]),
    )


def from_partners(value_for, subs):
    received = [value_for(0)]
    for hop in range(1, subs):
        received.append(lax.ppermute(value_for(hop), "sub", [(i, i ^ hop) for i in range(subs)]))
    return jnp.stack(received)


def gather_rows(rows, subs):
    received = from_partners(lambda hop: rows, subs)
    order = lax.axis_index("sub") ^ jnp.arange(subs, dtype=jnp.int32)
    return received[order].reshape((subs * rows.shape[0],) + rows.shape[1:])


def broadcast_rows(rows, subs):
    copies = jnp.broadcast_to(rows[None], (subs,) + rows.shape)
    pieces = lax.all_to_all(copies, "sub", 0, 0, tiled=True)
    return pieces.reshape((subs * rows.shape[0],) + rows.shape[1:])


def scatter_sum(blocks, subs):
    own = lax.axis_index("sub")
    received = from_partners(
        lambda hop: lax.dynamic_index_in_dim(blocks, own ^ hop, 0, keepdims=False), subs
    )
    return jnp.sum(received.astype(jnp.float32), axis=0)


def local(
    excitation,
    local_inverse,
    aggregation,
    disaggregation,
    translation,
    partners,
    list_counts,
    sweep_order,
):
    chips = lax.axis_size("zx")
    excite_rows = excitation[0]
    inverse_rows = local_inverse[0]
    agg_columns = aggregation[0]
    disagg_rows = disaggregation[0]
    trans_rows = translation[0]
    partner_row = partners[0]

    def apply_inverse(shard_rows):
        return jnp.dot(inverse_rows, shard_rows, preferred_element_type=jnp.float32)

    subs = lax.axis_size("sub")
    sub_index = lax.axis_index("sub")
    excite_parts = from_partners(lambda hop: excite_rows, subs)
    excite_block = excite_rows.shape[0]
    solved = jnp.zeros((inverse_rows.shape[0], excite_rows.shape[1]), jnp.float32)
    for hop in range(subs):
        columns = lax.dynamic_slice_in_dim(
            inverse_rows, (sub_index ^ hop) * excite_block, excite_block, axis=1
        )
        solved = solved + jnp.dot(columns, excite_parts[hop], preferred_element_type=jnp.float32)
    solved_half = solved.astype(jnp.bfloat16)
    partial_incident = lax.dot_general(
        solved_half, agg_columns, CONTRACT_FIRST, preferred_element_type=jnp.float32
    ).astype(jnp.bfloat16)
    incident = scatter_sum(partial_incident.reshape((subs, -1) + partial_incident.shape[1:]), subs)
    spread = apply_inverse(lax.all_gather(disagg_rows, "sub", axis=0, tiled=True))
    spread_half = spread.astype(jnp.bfloat16)
    partial_map = lax.dot_general(
        spread_half, agg_columns, CONTRACT_FIRST, preferred_element_type=jnp.float32
    ).astype(jnp.bfloat16)
    coupling = lax.psum(partial_map, "sub")

    domains = sweep_order.shape[0]
    members = domains // SEGMENTS
    segment_of = sweep_order * SEGMENTS // domains
    own_index = lax.axis_index("zx") * CORES + lax.axis_index("core")
    my_segment = segment_of[own_index]
    my_slot = sweep_order[own_index] - my_segment * members
    slot_ids = jnp.arange(members, dtype=jnp.int32)
    slot_live = jnp.arange(partner_row.shape[0], dtype=jnp.int32) < list_counts[0]
    partner_pos = sweep_order[partner_row]
    partner_segment = partner_pos * SEGMENTS // domains
    partner_slot = partner_pos - partner_segment * members

    half_samples = trans_rows.shape[-1] // LANES
    trans_tiles = trans_rows.reshape(trans_rows.shape[:2] + (half_samples, 1, LANES))
    incoming = jnp.zeros(to_tiles(incident).shape, jnp.float32)
    for segment_k in range(SEGMENTS - 1):
        if segment_k == 0:
            pattern = incident.astype(jnp.bfloat16)
        elif segment_k == 1:
            all_fields = broadcast_rows(from_tiles(incoming).astype(jnp.bfloat16), subs)
            products = jnp.dot(all_fields, partial_map, preferred_element_type=jnp.float32)
            coupled = scatter_sum(products.reshape((subs, -1) + products.shape[1:]), subs)
            pattern = (incident - coupled).astype(jnp.bfloat16)
        else:
            pattern = (
                incident
                - jnp.dot(
                    from_tiles(incoming).astype(jnp.bfloat16),
                    coupling,
                    preferred_element_type=jnp.float32,
                )
            ).astype(jnp.bfloat16)
        mine = (slot_ids == my_slot) & (my_segment == segment_k)
        pattern_tiles = to_tiles(pattern)
        slots = jnp.where(
            mine[:, None, None, None], pattern_tiles[None], jnp.zeros_like(pattern_tiles)[None]
        )
        slots = share_slots(slots, chips).astype(jnp.float32)
        match = (
            (partner_slot[:, None] == slot_ids[None, :])
            & (partner_segment[:, None] == segment_k)
            & slot_live[:, None]
            & (segment_k < my_segment)
        )
        weights = jnp.sum(
            jnp.where(match[:, :, None, None, None, None], trans_tiles[:, None], 0.0), axis=0
        )
        real_weight = weights[:, 0]
        imag_weight = weights[:, 1]
        real_part = slots[:, :half_samples]
        imag_part = slots[:, half_samples:]
        incoming = incoming + jnp.concatenate(
            [
                jnp.sum(real_weight * real_part - imag_weight * imag_part, axis=0),
                jnp.sum(real_weight * imag_part + imag_weight * real_part, axis=0),
            ],
            axis=0,
        )
    incoming = from_tiles(incoming)
    fields = gather_rows(incoming.astype(jnp.bfloat16), subs)
    currents = solved - lax.dot_general(
        spread_half, fields, CONTRACT_LAST, preferred_element_type=jnp.float32
    )
    return currents[None]


def solution(mesh):
    dom_size, sub_size = mesh.devices.shape
    fine = Mesh(mesh.devices.reshape(dom_size // CORES, CORES, sub_size), ("zx", "core", "sub"))
    in_specs = (
        P(DOM, "sub", None),
        P(DOM, "sub", None),
        P(DOM, None, "sub"),
        P(DOM, "sub", None),
        P(DOM, None, None, None),
        P(DOM, None),
        P(DOM),
        P(),
    )
    out_specs = P(DOM, "sub", None)
    return jax.shard_map(local, mesh=fine, in_specs=in_specs, out_specs=out_specs, check_vma=False)
```

```python
import jax
import jax.numpy as jnp
from jax import lax
from jax.sharding import Mesh
from jax.sharding import PartitionSpec as P

SEGMENTS = 8
CORES = 2


CONTRACT_FIRST = (((0,), (1,)), ((), ()))
CONTRACT_LAST = (((1,), (1,)), ((), ()))
DOM = ("zx", "core")
LANES = 128


def to_tiles(rows):
    lead = rows.shape[:-2]
    count, width = rows.shape[-2:]
    tiled = rows.reshape(lead + (count, width // LANES, LANES))
    return jnp.moveaxis(tiled, -2, -3)


def from_tiles(tiles):
    lead = tiles.shape[:-3]
    groups, count, lanes = tiles.shape[-3:]
    return jnp.moveaxis(tiles, -3, -2).reshape(lead + (count, groups * lanes))


def share_slots(slots, chips):
    swap = [(0, 1), (1, 0)]
    core = lax.axis_index("core")
    count = slots.shape[0]
    halves = slots.reshape((CORES, count // CORES) + slots.shape[1:])
    wanted = lax.dynamic_index_in_dim(halves, 1 - core, 0, keepdims=False)
    mine = lax.dynamic_index_in_dim(halves, core, 0, keepdims=False)
    mine = mine + lax.ppermute(wanted, "core", swap)
    tile_shape = mine.shape[2:]
    pieces = lax.all_to_all(mine.reshape((chips,) + tile_shape), "zx", 0, 0, tiled=True)
    total = jnp.sum(pieces, axis=0, keepdims=True)
    spread = jnp.broadcast_to(total, (chips,) + tile_shape)
    gathered = lax.all_to_all(spread, "zx", 0, 0, tiled=True).reshape(mine.shape)
    other = lax.ppermute(gathered, "core", swap)
    return jnp.concatenate([gathered, other])


def from_partners(value_for, subs):
    received = [value_for(0)]
    for hop in range(1, subs):
        received.append(lax.ppermute(value_for(hop), "sub", [(i, i ^ hop) for i in range(subs)]))
    return jnp.stack(received)


def gather_rows(rows, subs):
    received = from_partners(lambda hop: rows, subs)
    order = lax.axis_index("sub") ^ jnp.arange(subs, dtype=jnp.int32)
    return received[order].reshape((subs * rows.shape[0],) + rows.shape[1:])


def broadcast_rows(rows, subs):
    copies = jnp.broadcast_to(rows[None], (subs,) + rows.shape)
    pieces = lax.all_to_all(copies, "sub", 0, 0, tiled=True)
    return pieces.reshape((subs * rows.shape[0],) + rows.shape[1:])


def scatter_sum(blocks, subs):
    own = lax.axis_index("sub")
    received = from_partners(
        lambda hop: lax.dynamic_index_in_dim(blocks, own ^ hop, 0, keepdims=False), subs
    )
    return jnp.sum(received.astype(jnp.float32), axis=0)


def local(
    excitation,
    local_inverse,
    aggregation,
    disaggregation,
    translation,
    partners,
    list_counts,
    sweep_order,
):
    chips = lax.axis_size("zx")
    excite_rows = excitation[0]
    inverse_rows = local_inverse[0]
    agg_columns = aggregation[0]
    disagg_rows = disaggregation[0]
    trans_rows = translation[0]
    partner_row = partners[0]

    def apply_inverse(shard_rows):
        return jnp.dot(inverse_rows, shard_rows, preferred_element_type=jnp.float32)

    subs = lax.axis_size("sub")
    solved = apply_inverse(broadcast_rows(excite_rows, subs))
    solved_half = solved.astype(jnp.bfloat16)
    partial_incident = lax.dot_general(
        solved_half, agg_columns, CONTRACT_FIRST, preferred_element_type=jnp.float32
    ).astype(jnp.bfloat16)
    incident = scatter_sum(partial_incident.reshape((subs, -1) + partial_incident.shape[1:]), subs)
    spread = apply_inverse(lax.all_gather(disagg_rows, "sub", axis=0, tiled=True))
    spread_half = spread.astype(jnp.bfloat16)
    partial_map = lax.dot_general(
        spread_half, agg_columns, CONTRACT_FIRST, preferred_element_type=jnp.float32
    ).astype(jnp.bfloat16)
    coupling = lax.psum(partial_map, "sub")

    domains = sweep_order.shape[0]
    members = domains // SEGMENTS
    segment_of = sweep_order * SEGMENTS // domains
    own_index = lax.axis_index("zx") * CORES + lax.axis_index("core")
    my_segment = segment_of[own_index]
    my_slot = sweep_order[own_index] - my_segment * members
    slot_ids = jnp.arange(members, dtype=jnp.int32)
    slot_live = jnp.arange(partner_row.shape[0], dtype=jnp.int32) < list_counts[0]
    partner_pos = sweep_order[partner_row]
    partner_segment = partner_pos * SEGMENTS // domains
    partner_slot = partner_pos - partner_segment * members

    half_samples = trans_rows.shape[-1] // LANES
    trans_tiles = trans_rows.reshape(trans_rows.shape[:2] + (half_samples, 1, LANES))
    incoming = jnp.zeros(to_tiles(incident).shape, jnp.float32)
    for segment_k in range(SEGMENTS - 1):
        if segment_k == 0:
            pattern = incident.astype(jnp.bfloat16)
        elif segment_k == 1:
            all_fields = gather_rows(from_tiles(incoming).astype(jnp.bfloat16), subs)
            products = jnp.dot(all_fields, partial_map, preferred_element_type=jnp.float32)
            coupled = scatter_sum(products.reshape((subs, -1) + products.shape[1:]), subs)
            pattern = (incident - coupled).astype(jnp.bfloat16)
        else:
            pattern = (
                incident
                - jnp.dot(
                    from_tiles(incoming).astype(jnp.bfloat16),
                    coupling,
                    preferred_element_type=jnp.float32,
                )
            ).astype(jnp.bfloat16)
        mine = (slot_ids == my_slot) & (my_segment == segment_k)
        pattern_tiles = to_tiles(pattern)
        slots = jnp.where(
            mine[:, None, None, None], pattern_tiles[None], jnp.zeros_like(pattern_tiles)[None]
        )
        slots = share_slots(slots, chips).astype(jnp.float32)
        match = (
            (partner_slot[:, None] == slot_ids[None, :])
            & (partner_segment[:, None] == segment_k)
            & slot_live[:, None]
            & (segment_k < my_segment)
        )
        weights = jnp.sum(
            jnp.where(match[:, :, None, None, None, None], trans_tiles[:, None], 0.0), axis=0
        )
        weight_halves = weights.reshape((CORES, members // CORES) + weights.shape[1:])
        core = lax.axis_index("core")
        weights = jnp.concatenate(
            [
                lax.dynamic_index_in_dim(weight_halves, core, 0, keepdims=False),
                lax.dynamic_index_in_dim(weight_halves, 1 - core, 0, keepdims=False),
            ]
        )
        real_weight = weights[:, 0]
        imag_weight = weights[:, 1]
        real_part = slots[:, :half_samples]
        imag_part = slots[:, half_samples:]
        incoming = incoming + jnp.concatenate(
            [
                jnp.sum(real_weight * real_part - imag_weight * imag_part, axis=0),
                jnp.sum(real_weight * imag_part + imag_weight * real_part, axis=0),
            ],
            axis=0,
        )
    incoming = from_tiles(incoming)
    fields = gather_rows(incoming.astype(jnp.bfloat16), subs)
    currents = solved - lax.dot_general(
        spread_half, fields, CONTRACT_LAST, preferred_element_type=jnp.float32
    )
    return currents[None]


def solution(mesh):
    dom_size, sub_size = mesh.devices.shape
    fine = Mesh(mesh.devices.reshape(dom_size // CORES, CORES, sub_size), ("zx", "core", "sub"))
    in_specs = (
        P(DOM, "sub", None),
        P(DOM, "sub", None),
        P(DOM, None, "sub"),
        P(DOM, "sub", None),
        P(DOM, None, None, None),
        P(DOM, None),
        P(DOM),
        P(),
    )
    out_specs = P(DOM, "sub", None)
    return jax.shard_map(local, mesh=fine, in_specs=in_specs, out_specs=out_specs, check_vma=False)
```

```python
import jax
import jax.numpy as jnp
from jax import lax
from jax.sharding import Mesh
from jax.sharding import PartitionSpec as P

SEGMENTS = 8
CORES = 2


CONTRACT_FIRST = (((0,), (1,)), ((), ()))
CONTRACT_LAST = (((1,), (1,)), ((), ()))
DOM = ("zx", "core")
LANES = 128


def to_tiles(rows):
    lead = rows.shape[:-2]
    count, width = rows.shape[-2:]
    tiled = rows.reshape(lead + (count, width // LANES, LANES))
    return jnp.moveaxis(tiled, -2, -3)


def from_tiles(tiles):
    lead = tiles.shape[:-3]
    groups, count, lanes = tiles.shape[-3:]
    return jnp.moveaxis(tiles, -3, -2).reshape(lead + (count, groups * lanes))


def share_slots(slots, chips):
    swap = [(0, 1), (1, 0)]
    core = lax.axis_index("core")
    count = slots.shape[0]
    halves = slots.reshape((CORES, count // CORES) + slots.shape[1:])
    wanted = lax.dynamic_index_in_dim(halves, 1 - core, 0, keepdims=False)
    mine = lax.dynamic_index_in_dim(halves, core, 0, keepdims=False)
    mine = mine + lax.ppermute(wanted, "core", swap)
    tile_shape = mine.shape[2:]
    pieces = lax.all_to_all(mine.reshape((chips,) + tile_shape), "zx", 0, 0, tiled=True)
    total = jnp.sum(pieces, axis=0, keepdims=True)
    spread = jnp.broadcast_to(total, (chips,) + tile_shape)
    gathered = lax.all_to_all(spread, "zx", 0, 0, tiled=True).reshape(mine.shape)
    other = lax.ppermute(gathered, "core", swap)
    return jnp.where(
        core == 0,
        jnp.concatenate([gathered, other]),
        jnp.concatenate([other, gathered]),
    )


def from_partners(value_for, subs):
    received = [value_for(0)]
    for hop in range(1, subs):
        received.append(lax.ppermute(value_for(hop), "sub", [(i, i ^ hop) for i in range(subs)]))
    return jnp.stack(received)


def gather_rows(rows, subs):
    received = from_partners(lambda hop: rows, subs)
    order = lax.axis_index("sub") ^ jnp.arange(subs, dtype=jnp.int32)
    return received[order].reshape((subs * rows.shape[0],) + rows.shape[1:])


def broadcast_rows(rows, subs):
    copies = jnp.broadcast_to(rows[None], (subs,) + rows.shape)
    pieces = lax.all_to_all(copies, "sub", 0, 0, tiled=True)
    return pieces.reshape((subs * rows.shape[0],) + rows.shape[1:])


def scatter_sum(blocks, subs):
    own = lax.axis_index("sub")
    received = from_partners(
        lambda hop: lax.dynamic_index_in_dim(blocks, own ^ hop, 0, keepdims=False), subs
    )
    return jnp.sum(received.astype(jnp.float32), axis=0)


def local(
    excitation,
    local_inverse,
    aggregation,
    disaggregation,
    translation,
    partners,
    list_counts,
    sweep_order,
):
    chips = lax.axis_size("zx")
    excite_rows = excitation[0]
    inverse_rows = local_inverse[0]
    agg_columns = aggregation[0]
    disagg_rows = disaggregation[0]
    trans_rows = translation[0]
    partner_row = partners[0]

    def apply_inverse(shard_rows):
        return jnp.dot(inverse_rows, shard_rows, preferred_element_type=jnp.float32)

    subs = lax.axis_size("sub")
    solved = apply_inverse(broadcast_rows(excite_rows, subs))
    solved_half = solved.astype(jnp.bfloat16)
    partial_incident = lax.dot_general(
        solved_half, agg_columns, CONTRACT_FIRST, preferred_element_type=jnp.float32
    ).astype(jnp.bfloat16)
    incident = scatter_sum(partial_incident.reshape((subs, -1) + partial_incident.shape[1:]), subs)
    spread = apply_inverse(lax.all_gather(disagg_rows, "sub", axis=0, tiled=True))
    spread_half = spread.astype(jnp.bfloat16)
    partial_map = lax.dot_general(
        spread_half, agg_columns, CONTRACT_FIRST, preferred_element_type=jnp.float32
    ).astype(jnp.bfloat16)
    coupling = lax.psum(partial_map, "sub")

    domains = sweep_order.shape[0]
    members = domains // SEGMENTS
    segment_of = sweep_order * SEGMENTS // domains
    own_index = lax.axis_index("zx") * CORES + lax.axis_index("core")
    my_segment = segment_of[own_index]
    my_slot = sweep_order[own_index] - my_segment * members
    slot_ids = jnp.arange(members, dtype=jnp.int32)
    slot_live = jnp.arange(partner_row.shape[0], dtype=jnp.int32) < list_counts[0]
    partner_pos = sweep_order[partner_row]
    partner_segment = partner_pos * SEGMENTS // domains
    partner_slot = partner_pos - partner_segment * members

    half_samples = trans_rows.shape[-1] // LANES
    trans_tiles = trans_rows.reshape(trans_rows.shape[:2] + (half_samples, 1, LANES))
    incoming = jnp.zeros(to_tiles(incident).shape, jnp.float32)
    for segment_k in range(SEGMENTS - 1):
        if segment_k == 0:
            pattern = incident.astype(jnp.bfloat16)
        elif segment_k == 1:
            all_fields = gather_rows(from_tiles(incoming).astype(jnp.bfloat16), subs)
            products = jnp.dot(all_fields, partial_map, preferred_element_type=jnp.float32).astype(
                jnp.bfloat16
            )
            coupled = scatter_sum(products.reshape((subs, -1) + products.shape[1:]), subs)
            pattern = (incident - coupled).astype(jnp.bfloat16)
        else:
            pattern = (
                incident
                - jnp.dot(
                    from_tiles(incoming).astype(jnp.bfloat16),
                    coupling,
                    preferred_element_type=jnp.float32,
                )
            ).astype(jnp.bfloat16)
        mine = (slot_ids == my_slot) & (my_segment == segment_k)
        pattern_tiles = to_tiles(pattern)
        slots = jnp.where(
            mine[:, None, None, None], pattern_tiles[None], jnp.zeros_like(pattern_tiles)[None]
        )
        slots = share_slots(slots, chips).astype(jnp.float32)
        match = (
            (partner_slot[:, None] == slot_ids[None, :])
            & (partner_segment[:, None] == segment_k)
            & slot_live[:, None]
            & (segment_k < my_segment)
        )
        weights = jnp.sum(
            jnp.where(match[:, :, None, None, None, None], trans_tiles[:, None], 0.0), axis=0
        )
        real_weight = weights[:, 0]
        imag_weight = weights[:, 1]
        real_part = slots[:, :half_samples]
        imag_part = slots[:, half_samples:]
        incoming = incoming + jnp.concatenate(
            [
                jnp.sum(real_weight * real_part - imag_weight * imag_part, axis=0),
                jnp.sum(real_weight * imag_part + imag_weight * real_part, axis=0),
            ],
            axis=0,
        )
    incoming = from_tiles(incoming)
    fields = gather_rows(incoming.astype(jnp.bfloat16), subs)
    currents = solved - lax.dot_general(
        spread_half, fields, CONTRACT_LAST, preferred_element_type=jnp.float32
    )
    return currents[None]


def solution(mesh):
    dom_size, sub_size = mesh.devices.shape
    fine = Mesh(mesh.devices.reshape(dom_size // CORES, CORES, sub_size), ("zx", "core", "sub"))
    in_specs = (
        P(DOM, "sub", None),
        P(DOM, "sub", None),
        P(DOM, None, "sub"),
        P(DOM, "sub", None),
        P(DOM, None, None, None),
        P(DOM, None),
        P(DOM),
        P(),
    )
    out_specs = P(DOM, "sub", None)
    return jax.shard_map(local, mesh=fine, in_specs=in_specs, out_specs=out_specs, check_vma=False)
```
